128 devices in a mesh: seq: 16 (over x, z), head: 8 (over y, core).
Axes of the slice: x: 4, y: 4, z: 4, core: 2. Of those that a mesh axis runs over, the one named last changes fastest.
Arguments:
- own_rows: bfloat16 [16384, 2048], P('seq'), may hold values from -400 to 400
- gain: float32 [2048], replicated, may hold values from 0.1 to 1.9
- w_query: bfloat16 [2048, 2048], P(None, 'head'), may hold values from -1 to 1
- w_key: bfloat16 [2048, 2048], P(None, 'head'), may hold values from -1 to 1
- w_value: bfloat16 [2048, 2048], P(None, 'head'), may hold values from -0.125 to 0.125
- grad_context: bfloat16 [16384, 2048], P('seq', 'head'), may hold values from -6 to 6
- send_slot: int32 [16384], P('seq'), may hold values from 0 to 2047, as said below
- recv_slot: int32 [16384], P('seq'), may hold values from 0 to 2047, as said below
- episode_start: int32 [16384], P('seq'), may hold values from 0 to 16256, as said below
Outputs:
- context: bfloat16 [16384, 2048], P('seq', 'head')
- d_rows: bfloat16 [16384, 2048], P(('seq', 'head'))
The draws below stay inside these ranges and needn't reach their ends.
Inputs may be any that keep to these rules, and one draw needn't show every extreme that they name: `send_slot`: each owner's rows name distinct slots of its send buffer, which holds one bucket of 128 slots for each shard in shard order; slot b * 128 + c sends the row to shard b. At most 128 rows of one owner go to one shard, and in every draw some owner sends exactly 128 rows to some shard. `recv_slot`: A shard receives from each owner o the bucket meant for it at o * 128; each packed row names a distinct received slot that carries a row, so that every owner's row lands in exactly one packed row. `episode_start`: episodes are runs of consecutive packed rows whose starts are multiples of 128; a row's value is its episode's first row, at most the row and more than the row minus 1024. Every shard's first row belongs to an episode that began in the shard before it (the first shard aside). Every draw holds an episode of 8 blocks.
All inputs are finite; a program needn't handle non-finite values.
Results may differ from the reference program's by a relative error of at most 0.02.
The reference program's roundings to bfloat16 on the way (of `packed`, `normed`, `probs_low`, `grad_scores` and `grad_queries`) count: a program that leaves them out, or rounds other values in their place, can miss the bound.
Values may be sent and summed in bfloat16 or wider, within the bound.
No kernel may reach another device: no remote copies, remote signals or barrier semaphores. Data moves between devices by JAX's collectives and lax.ppermute only.
A program may use at most 128 MiB of HBM per device.

```python
import math
import jax
import jax.numpy as jnp
from jax import lax

D = 2048
H = 16
HD = 128
ROWS_DEV = 1024
BLOCK = 128
CAP = 128
TOTAL = 16384
N_SEQ = 16
N_HEAD = 8


def packing_tables(key):
    base_key = jax.random.fold_in(key, 7)
    order_key, send_key, recv_key = jax.random.split(base_key, 3)
    shards = N_SEQ
    share_rows = ROWS_DEV // shards
    capacity = 2 * share_rows
    chain_order = jax.random.permutation(order_key, shards)
    owners = jnp.arange(shards)
    counts = jnp.full((shards, shards), share_rows, jnp.int32)
    counts = counts.at[owners, chain_order].add(share_rows)
    counts = counts.at[owners, jnp.roll(chain_order, -1)].add(-share_rows)
    positions = jnp.arange(ROWS_DEV)
    send_ends = jnp.cumsum(counts, axis=1)
    target = jax.vmap(lambda row_ends: jnp.searchsorted(row_ends, positions, side='right'))(send_ends)
    within = positions[None, :] - jnp.take_along_axis(send_ends - counts, target, axis=1)
    send_order = jax.vmap(lambda sub_key: jax.random.permutation(sub_key, ROWS_DEV))(jax.random.split(send_key, shards))
    send_slot = jnp.zeros((shards, ROWS_DEV), jnp.int32).at[owners[:, None], send_order].set((target * capacity + within).astype(jnp.int32))
    recv_ends = jnp.cumsum(counts, axis=0).T
    source = jax.vmap(lambda row_ends: jnp.searchsorted(row_ends, positions, side='right'))(recv_ends)
    within_recv = positions[None, :] - jnp.take_along_axis(recv_ends - counts.T, source, axis=1)
    recv_order = jax.vmap(lambda sub_key: jax.random.permutation(sub_key, ROWS_DEV))(jax.random.split(recv_key, shards))
    recv_slot = jnp.zeros((shards, ROWS_DEV), jnp.int32).at[owners[:, None], recv_order].set((source * capacity + within_recv).astype(jnp.int32))
    return (send_slot.reshape(-1), recv_slot.reshape(-1))


def draw_send_slot(key, part):
    return packing_tables(key)[0]


def draw_recv_slot(key, part):
    return packing_tables(key)[1]


def draw_episode_start(key, part):
    before_key, after_key, flag_key, pick_key = jax.random.split(jax.random.fold_in(key, 13), 4)
    block_count = TOTAL // BLOCK
    most_blocks = ROWS_DEV // BLOCK
    half_blocks = most_blocks // 2
    bound_count = N_SEQ - 1
    before = jax.random.randint(before_key, (bound_count,), 1, half_blocks + 1)
    after = jax.random.randint(after_key, (bound_count,), 1, half_blocks + 1)
    chosen = jax.random.randint(pick_key, (), 0, bound_count)
    bound_ids = jnp.arange(bound_count, dtype=jnp.int32)
    before = jnp.where(bound_ids == chosen, half_blocks, before)
    after = jnp.where(bound_ids == chosen, half_blocks, after)
    edges = (bound_ids + 1) * most_blocks
    opens = edges - before
    closes = edges + after
    blocks = jnp.arange(block_count, dtype=jnp.int32)
    flags = jax.random.randint(flag_key, (block_count,), 0, 2) == 1
    inside = jnp.any((blocks[None, :] > opens[:, None]) & (blocks[None, :] < closes[:, None]), axis=0)
    marked = jnp.any((blocks[None, :] == opens[:, None]) | (blocks[None, :] == closes[:, None]), axis=0)
    flags = flags & jnp.logical_not(inside) | marked | (blocks == 0)
    first_block = lax.cummax(jnp.where(flags, blocks, 0), axis=0)
    return jnp.repeat(first_block * BLOCK, BLOCK, total_repeat_length=TOTAL).astype(jnp.int32)


def draw_own_rows(key, part):
    noise_key, row_key, column_key = jax.random.split(jax.random.fold_in(key, 17), 3)
    column_scale = jnp.exp(jax.random.uniform(column_key, (1, D), jnp.float32) * math.log(10.0))
    noise = jnp.clip(jax.random.normal(noise_key, (TOTAL, D), jnp.float32), -4.0, 4.0)
    row_scale = jnp.exp(jax.random.uniform(row_key, (TOTAL, 1), jnp.float32) * math.log(10.0))
    return (noise * row_scale * column_scale).astype(jnp.bfloat16)


def projection_draw(key):
    entries = jnp.clip(jax.random.normal(key, (D, H * HD), jnp.float32), -4.0, 4.0)
    return jnp.clip(entries * D ** (-0.5), -1.0, 1.0).astype(jnp.bfloat16)


def draw_w_query(key, part):
    return projection_draw(jax.random.fold_in(key, 19))


def draw_w_key(key, part):
    return projection_draw(jax.random.fold_in(key, 23))


def block_levels(rng, dims, cuts, low, top_value):
    level = 1.0
    for position, blocks in cuts:
        draws = jax.random.uniform(jax.random.fold_in(jax.random.fold_in(rng, 6), position), (blocks,), jnp.float32, low / len(cuts), top_value / len(cuts))
        level = level * jnp.repeat(jnp.exp(draws), dims[position] // blocks).reshape((-1,) + (1,) * (len(dims) - 1 - position))
    return level


def normal_values(stream_key, shape, width, most, pieces=(), kind=jnp.bfloat16):
    values = jax.random.normal(stream_key, shape, jnp.float32) * width
    if len(pieces) > 0:
        values = block_levels(stream_key, shape, pieces, -0.22, 0.18) * values
    return jnp.clip(values, min=-most, max=most).astype(kind)


def setup_inputs(seed: int = 0) -> dict:
    arg_keys = jax.random.split(jax.random.key(seed), 10)
    own_rows = draw_own_rows(jax.random.fold_in(arg_keys[9], 71), 0)
    gain = jnp.clip(1.0 + 0.18 * jax.random.normal(arg_keys[1], (D,), jnp.float32), 0.1, 1.9)
    w_query = draw_w_query(jax.random.fold_in(arg_keys[9], 71), 0)
    w_key = draw_w_key(jax.random.fold_in(arg_keys[9], 71), 0)
    w_value = normal_values(arg_keys[4], (D, H * HD), D ** -0.5, 0.125, ((1, 8),))
    grad_context = normal_values(arg_keys[5], (TOTAL, H * HD), 1.0, 6.0, ((0, 16), (1, 8)))
    send_slot = draw_send_slot(jax.random.fold_in(arg_keys[9], 71), 0)
    recv_slot = draw_recv_slot(jax.random.fold_in(arg_keys[9], 71), 0)
    episode_start = draw_episode_start(jax.random.fold_in(arg_keys[9], 71), 0)
    return {"own_rows": own_rows, "gain": gain, "w_query": w_query, "w_key": w_key, "w_value": w_value, "grad_context": grad_context, "send_slot": send_slot, "recv_slot": recv_slot, "episode_start": episode_start}


neg_large = -1e+30
epsilon = 1e-05

def move_rows(own_rows, send_slot, recv_slot):
    bucket_width = N_SEQ * CAP
    owner_index = jnp.arange(TOTAL, dtype=jnp.int32) // ROWS_DEV
    source_key = send_slot // CAP * bucket_width + owner_index * CAP + send_slot % CAP
    table = jnp.zeros((N_SEQ * bucket_width,), jnp.int32).at[source_key].set(jnp.arange(TOTAL, dtype=jnp.int32))
    target_key = owner_index * bucket_width + recv_slot
    return own_rows[table[target_key]]

def block_terms(queries, keys_all, values_all, grad_ctx, starts, first_query, first_key):
    score_scale = HD ** (-0.5)
    query_pos = first_query + jnp.arange(queries.shape[0], dtype=jnp.int32)
    key_pos = first_key + jnp.arange(keys_all.shape[0], dtype=jnp.int32)
    allowed = (key_pos[None, :] >= starts[:, None]) & (key_pos[None, :] <= query_pos[:, None])
    query_f = queries.astype(jnp.float32)
    keys_f = keys_all.astype(jnp.float32)
    values_f = values_all.astype(jnp.float32)
    grad_f = grad_ctx.astype(jnp.float32)
    scores = jnp.einsum('bhe,khe->bhk', query_f, keys_f) * score_scale
    scores = jnp.where(allowed[:, None, :], scores, neg_large)
    row_top = lax.optimization_barrier(jnp.max(scores, axis=-1, keepdims=True))
    log_total = row_top + jnp.log(lax.optimization_barrier(jnp.sum(jnp.exp(scores - row_top), axis=-1, keepdims=True)))
    probs = jnp.exp(scores - log_total)
    probs_low = probs.astype(jnp.bfloat16).astype(jnp.float32)
    context = jnp.einsum('bhk,khe->bhe', probs_low, values_f)
    grad_probs = jnp.einsum('bhe,khe->bhk', grad_f, values_f)
    weighted = lax.optimization_barrier(jnp.sum(probs * grad_probs, axis=-1, keepdims=True))
    grad_scores = (probs * (grad_probs - weighted)).astype(jnp.bfloat16).astype(jnp.float32)
    grad_q = jnp.einsum('bhk,khe->bhe', grad_scores, keys_f) * score_scale
    grad_k = jnp.einsum('bhk,bhe->khe', grad_scores, query_f) * score_scale
    grad_v = jnp.einsum('bhk,bhe->khe', probs_low, grad_f)
    return (context, grad_q, grad_k, grad_v)

def reference(own_rows, gain, w_query, w_key, w_value, grad_context, send_slot, recv_slot, episode_start):
    packed = move_rows(own_rows, send_slot, recv_slot)
    rows_float = packed.astype(jnp.float32)
    inv_rms = lax.rsqrt(lax.optimization_barrier(jnp.mean(rows_float * rows_float, axis=-1, keepdims=True)) + epsilon)
    normed = (rows_float * inv_rms * gain).astype(jnp.bfloat16)
    queries = jnp.dot(normed, w_query, preferred_element_type=jnp.float32).astype(jnp.bfloat16).reshape(TOTAL, H, HD)
    keys = jnp.dot(normed, w_key, preferred_element_type=jnp.float32).astype(jnp.bfloat16).reshape(TOTAL, H, HD)
    values = jnp.dot(normed, w_value, preferred_element_type=jnp.float32).astype(jnp.bfloat16).reshape(TOTAL, H, HD)
    grad_heads = grad_context.reshape(TOTAL, H, HD)
    zero_rows = jnp.zeros((ROWS_DEV, H, HD), jnp.bfloat16)
    keys_pad = jnp.concatenate([zero_rows, keys], axis=0)
    values_pad = jnp.concatenate([zero_rows, values], axis=0)

    def one_shard(shard):
        first = shard * ROWS_DEV
        shard_queries = lax.dynamic_slice_in_dim(queries, first, ROWS_DEV, 0)
        shard_keys = lax.dynamic_slice_in_dim(keys_pad, first, 2 * ROWS_DEV, 0)
        shard_values = lax.dynamic_slice_in_dim(values_pad, first, 2 * ROWS_DEV, 0)
        shard_grads = lax.dynamic_slice_in_dim(grad_heads, first, ROWS_DEV, 0)
        starts = lax.dynamic_slice_in_dim(episode_start, first, ROWS_DEV, 0)
        return block_terms(shard_queries, shard_keys, shard_values, shard_grads, starts, first, first - ROWS_DEV)
    contexts, grad_q, grad_k, grad_v = lax.map(one_shard, jnp.arange(N_SEQ, dtype=jnp.int32))

    def combine(parts):
        later = lax.optimization_barrier(parts[1:, :ROWS_DEV].astype(jnp.bfloat16)).astype(jnp.float32)
        later = jnp.concatenate([later, jnp.zeros((1, ROWS_DEV, H, HD), jnp.float32)], axis=0)
        return (parts[:, ROWS_DEV:] + later).astype(jnp.bfloat16).reshape(TOTAL, H * HD)
    context = contexts.astype(jnp.bfloat16).reshape(TOTAL, H * HD)
    grad_queries = grad_q.astype(jnp.bfloat16).reshape(TOTAL, H * HD)
    grad_keys = combine(grad_k)
    grad_values = combine(grad_v)
    group_width = H * HD // N_HEAD
    grad_normed = jnp.zeros((TOTAL, D), jnp.float32)
    for group_index in range(N_HEAD):
        low = group_index * group_width
        high = low + group_width
        term = jnp.dot(grad_queries[:, low:high], w_query[:, low:high].T, preferred_element_type=jnp.float32)
        term = term + jnp.dot(grad_keys[:, low:high], w_key[:, low:high].T, preferred_element_type=jnp.float32)
        term = term + jnp.dot(grad_values[:, low:high], w_value[:, low:high].T, preferred_element_type=jnp.float32)
        grad_normed = grad_normed + lax.optimization_barrier(term.astype(jnp.bfloat16)).astype(jnp.float32)
    gain_grad = gain * grad_normed
    mixed = lax.optimization_barrier(jnp.mean(gain_grad * rows_float, axis=-1, keepdims=True))
    d_rows = (inv_rms * gain_grad - rows_float * inv_rms ** 3 * mixed).astype(jnp.bfloat16)
    return (context, d_rows)
```

```python
import jax
import jax.numpy as jnp
from jax import lax
from jax.sharding import PartitionSpec as P

HD = 128


neg_large = -1e30
epsilon = 1e-05


def passed_along(array, axis, by):
    count = lax.axis_size(axis)
    pairs = [(i, i + by) for i in range(count) if 0 <= i + by < count]
    return lax.ppermute(array, axis, pairs)


def block_terms(queries, keys_all, values_all, grad_ctx, starts, first_query, first_key):
    score_scale = queries.shape[-1] ** (-0.5)
    query_pos = first_query + jnp.arange(queries.shape[0], dtype=jnp.int32)
    key_pos = first_key + jnp.arange(keys_all.shape[0], dtype=jnp.int32)
    allowed = (key_pos[None, :] >= starts[:, None]) & (key_pos[None, :] <= query_pos[:, None])
    scores = (
        jnp.einsum("bhe,khe->bhk", queries, keys_all, preferred_element_type=jnp.float32)
        * score_scale
    )
    scores = jnp.where(allowed[:, None, :], scores, neg_large)
    row_top = jnp.max(scores, axis=-1, keepdims=True)
    log_total = row_top + jnp.log(jnp.sum(jnp.exp(scores - row_top), axis=-1, keepdims=True))
    probs = jnp.exp(scores - log_total)
    probs_low = probs.astype(jnp.bfloat16)
    context = jnp.einsum("bhk,khe->bhe", probs_low, values_all, preferred_element_type=jnp.float32)
    grad_probs = jnp.einsum(
        "bhe,khe->bhk", grad_ctx, values_all, preferred_element_type=jnp.float32
    )
    weighted = jnp.sum(probs * grad_probs, axis=-1, keepdims=True)
    grad_scores = (probs * (grad_probs - weighted)).astype(jnp.bfloat16)
    grad_q = (
        jnp.einsum("bhk,khe->bhe", grad_scores, keys_all, preferred_element_type=jnp.float32)
        * score_scale
    )
    grad_k = (
        jnp.einsum("bhk,bhe->khe", grad_scores, queries, preferred_element_type=jnp.float32)
        * score_scale
    )
    grad_v = jnp.einsum("bhk,bhe->khe", probs_low, grad_ctx, preferred_element_type=jnp.float32)
    return (context, grad_q, grad_k, grad_v)


def body(
    own_rows, gain, w_query, w_key, w_value, grad_context, send_slot, recv_slot, episode_start
):
    seq_count = lax.axis_size("seq")
    head_count = lax.axis_size("head")
    shard = lax.axis_index("seq")
    head_pos = lax.axis_index("head")
    row_count = own_rows.shape[0]
    capacity = 2 * row_count // seq_count
    width = own_rows.shape[1] // head_count
    own_part = lax.dynamic_slice_in_dim(own_rows, head_pos * width, width, 1)
    outgoing = (
        jnp.zeros((seq_count * capacity, width), own_rows.dtype)
        .at[send_slot]
        .set(own_part)
    )
    arrived = lax.all_to_all(outgoing, "seq", split_axis=0, concat_axis=0, tiled=True)
    packed_part = jnp.take(arrived, recv_slot, axis=0)
    packed = lax.all_gather(packed_part, "head", axis=1, tiled=True)
    rows_float = packed.astype(jnp.float32)
    inv_rms = lax.rsqrt(jnp.mean(rows_float * rows_float, axis=-1, keepdims=True) + epsilon)
    normed = (rows_float * inv_rms * gain).astype(jnp.bfloat16)
    queries = jnp.dot(normed, w_query, preferred_element_type=jnp.float32).astype(jnp.bfloat16)
    keys_own = jnp.dot(normed, w_key, preferred_element_type=jnp.float32).astype(jnp.bfloat16)
    values_own = jnp.dot(normed, w_value, preferred_element_type=jnp.float32).astype(jnp.bfloat16)
    keys_prev, values_prev = passed_along((keys_own, values_own), "seq", 1)
    local_heads = queries.shape[1] // HD

    def split_heads(matrix):
        return matrix.reshape(matrix.shape[0], local_heads, HD)

    keys_all = split_heads(jnp.concatenate([keys_prev, keys_own], axis=0))
    values_all = split_heads(jnp.concatenate([values_prev, values_own], axis=0))
    query_heads = split_heads(queries)
    grad_heads = split_heads(grad_context)
    block_rows = min(512, row_count)
    first_key = (shard - 1) * row_count
    contexts = []
    grad_queries = []
    grad_keys = jnp.zeros(keys_all.shape, jnp.float32)
    grad_values = jnp.zeros(values_all.shape, jnp.float32)
    for block_index in range(row_count // block_rows):
        low = block_index * block_rows
        high = low + block_rows
        context, grad_q, grad_k, grad_v = block_terms(
            query_heads[low:high],
            keys_all,
            values_all,
            grad_heads[low:high],
            episode_start[low:high],
            shard * row_count + low,
            first_key,
        )
        contexts.append(context.astype(jnp.bfloat16))
        grad_queries.append(grad_q.astype(jnp.bfloat16))
        grad_keys = grad_keys + grad_k
        grad_values = grad_values + grad_v
    context_out = jnp.concatenate(contexts, axis=0).reshape(row_count, -1)
    grad_q_all = jnp.concatenate(grad_queries, axis=0).reshape(row_count, -1)
    send_back = (
        grad_keys[:row_count].reshape(row_count, -1).astype(jnp.bfloat16),
        grad_values[:row_count].reshape(row_count, -1).astype(jnp.bfloat16),
    )
    next_keys, next_values = passed_along((send_back[0], send_back[1]), "seq", -1)
    grad_k_all = (
        grad_keys[row_count:].reshape(row_count, -1) + next_keys.astype(jnp.float32)
    ).astype(jnp.bfloat16)
    grad_v_all = (
        grad_values[row_count:].reshape(row_count, -1) + next_values.astype(jnp.float32)
    ).astype(jnp.bfloat16)
    share = row_count // head_count

    def project(grads, weight):
        return jnp.einsum("rc,dc->rd", grads, weight, preferred_element_type=jnp.float32)

    grad_normed = lax.psum_scatter(
        (
            project(grad_q_all, w_query) + project(grad_k_all, w_key) + project(grad_v_all, w_value)
        ).astype(jnp.bfloat16),
        "head",
        scatter_dimension=0,
        tiled=True,
    ).astype(jnp.float32)
    own_start = head_pos * share
    mine = lax.dynamic_slice_in_dim(rows_float, own_start, share, 0)
    mine_inv = lax.dynamic_slice_in_dim(inv_rms, own_start, share, 0)
    gain_grad = gain * grad_normed
    mixed = jnp.mean(gain_grad * mine, axis=-1, keepdims=True)
    d_rows = (mine_inv * gain_grad - mine * mine_inv**3 * mixed).astype(jnp.bfloat16)
    return (context_out, d_rows)


def solution(mesh):
    in_specs = (
        P("seq", None),
        P(),
        P(None, "head"),
        P(None, "head"),
        P(None, "head"),
        P("seq", "head"),
        P("seq"),
        P("seq"),
        P("seq"),
    )
    out_specs = (P("seq", "head"), P(("seq", "head"), None))
    return jax.shard_map(body, mesh=mesh, in_specs=in_specs, out_specs=out_specs, check_vma=False)
```

```python
import functools

import jax
import jax.numpy as jnp
from jax import lax
from jax.experimental import pallas as pl
from jax.experimental.pallas import tpu as pltpu
from jax.sharding import PartitionSpec as P

HD = 128


neg_large = -1e30
epsilon = 1e-05


def passed_along(array, axis, by):
    count = lax.axis_size(axis)
    pairs = [(i, i + by) for i in range(count) if 0 <= i + by < count]
    return lax.ppermute(array, axis, pairs)


def block_terms(queries, keys_all, values_all, grad_ctx, starts, first_query, first_key):
    score_scale = queries.shape[-1] ** (-0.5)
    query_pos = first_query + jnp.arange(queries.shape[0], dtype=jnp.int32)
    key_pos = first_key + jnp.arange(keys_all.shape[0], dtype=jnp.int32)
    allowed = (key_pos[None, :] >= starts[:, None]) & (key_pos[None, :] <= query_pos[:, None])
    scores = (
        jnp.einsum("bhe,khe->bhk", queries, keys_all, preferred_element_type=jnp.float32)
        * score_scale
    )
    scores = jnp.where(allowed[:, None, :], scores, neg_large)
    row_top = jnp.max(scores, axis=-1, keepdims=True)
    log_total = row_top + jnp.log(jnp.sum(jnp.exp(scores - row_top), axis=-1, keepdims=True))
    probs = jnp.exp(scores - log_total)
    probs_low = probs.astype(jnp.bfloat16)
    context = jnp.einsum("bhk,khe->bhe", probs_low, values_all, preferred_element_type=jnp.float32)
    grad_probs = jnp.einsum(
        "bhe,khe->bhk", grad_ctx, values_all, preferred_element_type=jnp.float32
    )
    weighted = jnp.sum(probs * grad_probs, axis=-1, keepdims=True)
    grad_scores = (probs * (grad_probs - weighted)).astype(jnp.bfloat16)
    grad_q = (
        jnp.einsum("bhk,khe->bhe", grad_scores, keys_all, preferred_element_type=jnp.float32)
        * score_scale
    )
    grad_k = (
        jnp.einsum("bhk,bhe->khe", grad_scores, queries, preferred_element_type=jnp.float32)
        * score_scale
    )
    grad_v = jnp.einsum("bhk,bhe->khe", probs_low, grad_ctx, preferred_element_type=jnp.float32)
    return (context, grad_q, grad_k, grad_v)


def attention_kernel(
    q_ref, k_ref, v_ref, do_ref, st_ref, ctx_ref, dq_ref, dk_ref, dv_ref, *, tq, window, shift, scale
):
    qi = pl.program_id(1)
    a = pl.multiple_of(qi * tq, tq)

    @pl.when(qi == 0)
    def _():
        dk_ref[...] = jnp.zeros_like(dk_ref)
        dv_ref[...] = jnp.zeros_like(dv_ref)

    q = q_ref[...]
    k = k_ref[pl.ds(a, window), :]
    v = v_ref[pl.ds(a, window), :]
    do = do_ref[...]
    rows_t = (((1,), (1,)), ((), ()))
    cols_t = (((0,), (0,)), ((), ()))
    s = lax.dot_general(q, k, rows_t, preferred_element_type=jnp.float32) * scale
    key_idx = a + lax.broadcasted_iota(jnp.int32, (tq, window), 1)
    row_idx = a + shift + lax.broadcasted_iota(jnp.int32, (tq, window), 0)
    allowed = (key_idx >= st_ref[...]) & (key_idx <= row_idx)
    s = jnp.where(allowed, s, neg_large)
    row_top = jnp.max(s, axis=1, keepdims=True)
    log_total = row_top + jnp.log(jnp.sum(jnp.exp(s - row_top), axis=1, keepdims=True))
    p = jnp.exp(s - log_total)
    p_low = p.astype(jnp.bfloat16)
    ctx_ref[...] = jnp.dot(p_low, v, preferred_element_type=jnp.float32).astype(ctx_ref.dtype)
    dp = lax.dot_general(do, v, rows_t, preferred_element_type=jnp.float32)
    weighted = jnp.sum(p * dp, axis=1, keepdims=True)
    ds = (p * (dp - weighted)).astype(jnp.bfloat16)
    dq_ref[...] = (jnp.dot(ds, k, preferred_element_type=jnp.float32) * scale).astype(dq_ref.dtype)
    dk_ref[pl.ds(a, window), :] += lax.dot_general(ds, q, cols_t, preferred_element_type=jnp.float32)
    dv_ref[pl.ds(a, window), :] += lax.dot_general(p_low, do, cols_t, preferred_element_type=jnp.float32)


def attention(queries, keys_all, values_all, grad_ctx, rel_start):
    rows, width = queries.shape
    heads = width // HD
    tq = 256
    window = rows + tq
    kernel = functools.partial(
        attention_kernel, tq=tq, window=window, shift=rows, scale=HD ** (-0.5)
    )
    q_spec = pl.BlockSpec((tq, HD), lambda h, i: (i, h))
    kv_spec = pl.BlockSpec((2 * rows, HD), lambda h, i: (0, h))
    steps = heads * (rows // tq)
    cost = pl.CostEstimate(
        flops=steps * 12 * tq * window * HD,
        transcendentals=steps * 2 * tq * window,
        bytes_accessed=rows * width * 2 * 4 + 2 * rows * width * (2 * 2 + 4 * 2),
    )
    return pl.pallas_call(
        kernel,
        grid=(heads, rows // tq),
        in_specs=[q_spec, kv_spec, kv_spec, q_spec, pl.BlockSpec((tq, 1), lambda h, i: (i, 0))],
        out_specs=[q_spec, q_spec, kv_spec, kv_spec],
        out_shape=[
            jax.ShapeDtypeStruct((rows, width), jnp.bfloat16),
            jax.ShapeDtypeStruct((rows, width), jnp.bfloat16),
            jax.ShapeDtypeStruct((2 * rows, width), jnp.float32),
            jax.ShapeDtypeStruct((2 * rows, width), jnp.float32),
        ],
        compiler_params=pltpu.CompilerParams(dimension_semantics=("arbitrary", "arbitrary")),
        cost_estimate=cost,
    )(queries, keys_all, values_all, grad_ctx, rel_start)


def body(
    own_rows, gain, w_query, w_key, w_value, grad_context, send_slot, recv_slot, episode_start
):
    seq_count = lax.axis_size("seq")
    head_count = lax.axis_size("head")
    shard = lax.axis_index("seq")
    head_pos = lax.axis_index("head")
    row_count = own_rows.shape[0]
    capacity = 2 * row_count // seq_count
    width = own_rows.shape[1] // head_count
    own_part = lax.dynamic_slice_in_dim(own_rows, head_pos * width, width, 1)
    outgoing = (
        jnp.zeros((seq_count * capacity, width), own_rows.dtype)
        .at[send_slot]
        .set(own_part)
    )
    arrived = lax.all_to_all(outgoing, "seq", split_axis=0, concat_axis=0, tiled=True)
    packed_part = jnp.take(arrived, recv_slot, axis=0)
    packed = lax.all_gather(packed_part, "head", axis=1, tiled=True)
    rows_float = packed.astype(jnp.float32)
    inv_rms = lax.rsqrt(jnp.mean(rows_float * rows_float, axis=-1, keepdims=True) + epsilon)
    normed = (rows_float * inv_rms * gain).astype(jnp.bfloat16)
    queries = jnp.dot(normed, w_query, preferred_element_type=jnp.float32).astype(jnp.bfloat16)
    keys_own = jnp.dot(normed, w_key, preferred_element_type=jnp.float32).astype(jnp.bfloat16)
    values_own = jnp.dot(normed, w_value, preferred_element_type=jnp.float32).astype(jnp.bfloat16)
    keys_prev, values_prev = passed_along((keys_own, values_own), "seq", 1)
    keys_all = jnp.concatenate([keys_prev, keys_own], axis=0)
    values_all = jnp.concatenate([values_prev, values_own], axis=0)
    rel_start = (episode_start - (shard - 1) * row_count).reshape(row_count, 1)
    context_out, grad_q_all, grad_keys, grad_values = attention(
        queries, keys_all, values_all, grad_context, rel_start
    )
    grad_keys = grad_keys * HD ** (-0.5)
    send_back = (
        grad_keys[:row_count].astype(jnp.bfloat16),
        grad_values[:row_count].astype(jnp.bfloat16),
    )
    next_keys, next_values = passed_along((send_back[0], send_back[1]), "seq", -1)
    grad_k_all = (
        grad_keys[row_count:] + next_keys.astype(jnp.float32)
    ).astype(jnp.bfloat16)
    grad_v_all = (
        grad_values[row_count:] + next_values.astype(jnp.float32)
    ).astype(jnp.bfloat16)
    share = row_count // head_count

    def project(grads, weight):
        return jnp.einsum("rc,dc->rd", grads, weight, preferred_element_type=jnp.float32)

    grad_normed = lax.psum_scatter(
        (
            project(grad_q_all, w_query) + project(grad_k_all, w_key) + project(grad_v_all, w_value)
        ).astype(jnp.bfloat16),
        "head",
        scatter_dimension=0,
        tiled=True,
    ).astype(jnp.float32)
    own_start = head_pos * share
    mine = lax.dynamic_slice_in_dim(rows_float, own_start, share, 0)
    mine_inv = lax.dynamic_slice_in_dim(inv_rms, own_start, share, 0)
    gain_grad = gain * grad_normed
    mixed = jnp.mean(gain_grad * mine, axis=-1, keepdims=True)
    d_rows = (mine_inv * gain_grad - mine * mine_inv**3 * mixed).astype(jnp.bfloat16)
    return (context_out, d_rows)


def solution(mesh):
    in_specs = (
        P("seq", None),
        P(),
        P(None, "head"),
        P(None, "head"),
        P(None, "head"),
        P("seq", "head"),
        P("seq"),
        P("seq"),
        P("seq"),
    )
    out_specs = (P("seq", "head"), P(("seq", "head"), None))
    return jax.shard_map(body, mesh=mesh, in_specs=in_specs, out_specs=out_specs, check_vma=False)
```

```python
import functools

import jax
import jax.numpy as jnp
from jax import lax
from jax.experimental import pallas as pl
from jax.experimental.pallas import tpu as pltpu
from jax.sharding import PartitionSpec as P

HD = 128


neg_large = -1e30
epsilon = 1e-05


def passed_along(array, axis, by):
    count = lax.axis_size(axis)
    pairs = [(i, i + by) for i in range(count) if 0 <= i + by < count]
    return lax.ppermute(array, axis, pairs)


def block_terms(queries, keys_all, values_all, grad_ctx, starts, first_query, first_key):
    score_scale = queries.shape[-1] ** (-0.5)
    query_pos = first_query + jnp.arange(queries.shape[0], dtype=jnp.int32)
    key_pos = first_key + jnp.arange(keys_all.shape[0], dtype=jnp.int32)
    allowed = (key_pos[None, :] >= starts[:, None]) & (key_pos[None, :] <= query_pos[:, None])
    scores = (
        jnp.einsum("bhe,khe->bhk", queries, keys_all, preferred_element_type=jnp.float32)
        * score_scale
    )
    scores = jnp.where(allowed[:, None, :], scores, neg_large)
    row_top = jnp.max(scores, axis=-1, keepdims=True)
    log_total = row_top + jnp.log(jnp.sum(jnp.exp(scores - row_top), axis=-1, keepdims=True))
    probs = jnp.exp(scores - log_total)
    probs_low = probs.astype(jnp.bfloat16)
    context = jnp.einsum("bhk,khe->bhe", probs_low, values_all, preferred_element_type=jnp.float32)
    grad_probs = jnp.einsum(
        "bhe,khe->bhk", grad_ctx, values_all, preferred_element_type=jnp.float32
    )
    weighted = jnp.sum(probs * grad_probs, axis=-1, keepdims=True)
    grad_scores = (probs * (grad_probs - weighted)).astype(jnp.bfloat16)
    grad_q = (
        jnp.einsum("bhk,khe->bhe", grad_scores, keys_all, preferred_element_type=jnp.float32)
        * score_scale
    )
    grad_k = (
        jnp.einsum("bhk,bhe->khe", grad_scores, queries, preferred_element_type=jnp.float32)
        * score_scale
    )
    grad_v = jnp.einsum("bhk,bhe->khe", probs_low, grad_ctx, preferred_element_type=jnp.float32)
    return (context, grad_q, grad_k, grad_v)


def attention_kernel(
    q_ref, k_ref, v_ref, do_ref, st_ref, ctx_ref, dq_ref, dk_ref, dv_ref, *, tq, window, shift, scale
):
    qi = pl.program_id(1)
    a = pl.multiple_of(qi * tq, tq)

    @pl.when(qi == 0)
    def _():
        dk_ref[...] = jnp.zeros_like(dk_ref)
        dv_ref[...] = jnp.zeros_like(dv_ref)

    q = q_ref[...]
    k = k_ref[pl.ds(a, window), :]
    v = v_ref[pl.ds(a, window), :]
    do = do_ref[...]
    rows_t = (((1,), (1,)), ((), ()))
    cols_t = (((0,), (0,)), ((), ()))
    s = lax.dot_general(q, k, rows_t, preferred_element_type=jnp.float32) * scale
    key_idx = a + lax.broadcasted_iota(jnp.int32, (tq, window), 1)
    row_idx = a + shift + lax.broadcasted_iota(jnp.int32, (tq, window), 0)
    allowed = (key_idx >= st_ref[...]) & (key_idx <= row_idx)
    s = jnp.where(allowed, s, neg_large)
    row_top = jnp.max(s, axis=1, keepdims=True)
    log_total = row_top + jnp.log(jnp.sum(jnp.exp(s - row_top), axis=1, keepdims=True))
    p = jnp.exp(s - log_total)
    p_low = p.astype(jnp.bfloat16)
    ctx_ref[...] = jnp.dot(p_low, v, preferred_element_type=jnp.float32).astype(ctx_ref.dtype)
    dp = lax.dot_general(do, v, rows_t, preferred_element_type=jnp.float32)
    weighted = jnp.sum(p * dp, axis=1, keepdims=True)
    ds = (p * (dp - weighted)).astype(jnp.bfloat16)
    dq_ref[...] = (jnp.dot(ds, k, preferred_element_type=jnp.float32) * scale).astype(dq_ref.dtype)
    dk_ref[pl.ds(a, window), :] += lax.dot_general(ds, q, cols_t, preferred_element_type=jnp.float32)
    dv_ref[pl.ds(a, window), :] += lax.dot_general(p_low, do, cols_t, preferred_element_type=jnp.float32)


def attention(queries, keys_all, values_all, grad_ctx, rel_start):
    rows, width = queries.shape
    heads = width // HD
    tq = 256
    window = rows + tq
    kernel = functools.partial(
        attention_kernel, tq=tq, window=window, shift=rows, scale=HD ** (-0.5)
    )
    q_spec = pl.BlockSpec((tq, HD), lambda h, i: (i, h))
    kv_spec = pl.BlockSpec((2 * rows, HD), lambda h, i: (0, h))
    steps = heads * (rows // tq)
    cost = pl.CostEstimate(
        flops=steps * 12 * tq * window * HD,
        transcendentals=steps * 2 * tq * window,
        bytes_accessed=rows * width * 2 * 4 + 2 * rows * width * (2 * 2 + 4 * 2),
    )
    return pl.pallas_call(
        kernel,
        grid=(heads, rows // tq),
        in_specs=[q_spec, kv_spec, kv_spec, q_spec, pl.BlockSpec((tq, 1), lambda h, i: (i, 0))],
        out_specs=[q_spec, q_spec, kv_spec, kv_spec],
        out_shape=[
            jax.ShapeDtypeStruct((rows, width), jnp.bfloat16),
            jax.ShapeDtypeStruct((rows, width), jnp.bfloat16),
            jax.ShapeDtypeStruct((2 * rows, width), jnp.float32),
            jax.ShapeDtypeStruct((2 * rows, width), jnp.float32),
        ],
        compiler_params=pltpu.CompilerParams(dimension_semantics=("arbitrary", "arbitrary")),
        cost_estimate=cost,
    )(queries, keys_all, values_all, grad_ctx, rel_start)


def body(
    own_rows, gain, w_query, w_key, w_value, grad_context, send_slot, recv_slot, episode_start
):
    seq_count = lax.axis_size("seq")
    chip_count = lax.axis_size("hy")
    core_count = lax.axis_size("hc")
    head_count = chip_count * core_count
    shard = lax.axis_index("seq")
    head_pos = lax.axis_index("hy") * core_count + lax.axis_index("hc")
    row_count = own_rows.shape[0]
    capacity = 2 * row_count // seq_count
    width = own_rows.shape[1] // head_count
    own_part = lax.dynamic_slice_in_dim(own_rows, head_pos * width, width, 1)
    outgoing = (
        jnp.zeros((seq_count * capacity, width), own_rows.dtype)
        .at[send_slot]
        .set(own_part)
    )
    arrived = lax.all_to_all(outgoing, "seq", split_axis=0, concat_axis=0, tiled=True)
    packed_part = jnp.take(arrived, recv_slot, axis=0)
    packed = lax.all_gather(packed_part, ("hy", "hc"), axis=1, tiled=True)
    rows_float = packed.astype(jnp.float32)
    inv_rms = lax.rsqrt(jnp.mean(rows_float * rows_float, axis=-1, keepdims=True) + epsilon)
    normed = (rows_float * inv_rms * gain).astype(jnp.bfloat16)
    queries = jnp.dot(normed, w_query, preferred_element_type=jnp.float32).astype(jnp.bfloat16)
    keys_own = jnp.dot(normed, w_key, preferred_element_type=jnp.float32).astype(jnp.bfloat16)
    values_own = jnp.dot(normed, w_value, preferred_element_type=jnp.float32).astype(jnp.bfloat16)
    keys_prev, values_prev = passed_along((keys_own, values_own), "seq", 1)
    keys_all = jnp.concatenate([keys_prev, keys_own], axis=0)
    values_all = jnp.concatenate([values_prev, values_own], axis=0)
    rel_start = (episode_start - (shard - 1) * row_count).reshape(row_count, 1)
    context_out, grad_q_all, grad_keys, grad_values = attention(
        queries, keys_all, values_all, grad_context, rel_start
    )
    grad_keys = grad_keys * HD ** (-0.5)
    send_back = (
        grad_keys[:row_count].astype(jnp.bfloat16),
        grad_values[:row_count].astype(jnp.bfloat16),
    )
    next_keys, next_values = passed_along((send_back[0], send_back[1]), "seq", -1)
    grad_k_all = (
        grad_keys[row_count:] + next_keys.astype(jnp.float32)
    ).astype(jnp.bfloat16)
    grad_v_all = (
        grad_values[row_count:] + next_values.astype(jnp.float32)
    ).astype(jnp.bfloat16)
    share = row_count // head_count

    def project(grads, weight):
        return jnp.einsum("rc,dc->rd", grads, weight, preferred_element_type=jnp.float32)

    term = (
        project(grad_q_all, w_query) + project(grad_k_all, w_key) + project(grad_v_all, w_value)
    ).astype(jnp.bfloat16)
    term = term.reshape(chip_count, core_count, share, -1).transpose(1, 0, 2, 3)
    term = term.reshape(row_count, -1)
    term = lax.psum_scatter(term, "hc", scatter_dimension=0, tiled=True)
    grad_normed = lax.psum_scatter(term, "hy", scatter_dimension=0, tiled=True).astype(jnp.float32)
    own_start = head_pos * share
    mine = lax.dynamic_slice_in_dim(rows_float, own_start, share, 0)
    mine_inv = lax.dynamic_slice_in_dim(inv_rms, own_start, share, 0)
    gain_grad = gain * grad_normed
    mixed = jnp.mean(gain_grad * mine, axis=-1, keepdims=True)
    d_rows = (mine_inv * gain_grad - mine * mine_inv**3 * mixed).astype(jnp.bfloat16)
    return (context_out, d_rows)


def solution(mesh):
    seq_count, head_count = mesh.devices.shape
    core_count = 2
    split_mesh = jax.sharding.Mesh(
        mesh.devices.reshape(seq_count, head_count // core_count, core_count), ("seq", "hy", "hc")
    )
    head = ("hy", "hc")
    in_specs = (
        P("seq", None),
        P(),
        P(None, head),
        P(None, head),
        P(None, head),
        P("seq", head),
        P("seq"),
        P("seq"),
        P("seq"),
    )
    out_specs = (P("seq", head), P(("seq",) + head, None))
    return jax.shard_map(
        body, mesh=split_mesh, in_specs=in_specs, out_specs=out_specs, check_vma=False
    )
```

```python
import functools

import jax
import jax.numpy as jnp
from jax import lax
from jax.experimental import pallas as pl
from jax.experimental.pallas import tpu as pltpu
from jax.sharding import PartitionSpec as P

HD = 128


neg_large = -1e30
epsilon = 1e-05


def passed_along(array, axis, by):
    count = lax.axis_size(axis)
    pairs = [(i, i + by) for i in range(count) if 0 <= i + by < count]
    return lax.ppermute(array, axis, pairs)


def block_terms(queries, keys_all, values_all, grad_ctx, starts, first_query, first_key):
    score_scale = queries.shape[-1] ** (-0.5)
    query_pos = first_query + jnp.arange(queries.shape[0], dtype=jnp.int32)
    key_pos = first_key + jnp.arange(keys_all.shape[0], dtype=jnp.int32)
    allowed = (key_pos[None, :] >= starts[:, None]) & (key_pos[None, :] <= query_pos[:, None])
    scores = (
        jnp.einsum("bhe,khe->bhk", queries, keys_all, preferred_element_type=jnp.float32)
        * score_scale
    )
    scores = jnp.where(allowed[:, None, :], scores, neg_large)
    row_top = jnp.max(scores, axis=-1, keepdims=True)
    log_total = row_top + jnp.log(jnp.sum(jnp.exp(scores - row_top), axis=-1, keepdims=True))
    probs = jnp.exp(scores - log_total)
    probs_low = probs.astype(jnp.bfloat16)
    context = jnp.einsum("bhk,khe->bhe", probs_low, values_all, preferred_element_type=jnp.float32)
    grad_probs = jnp.einsum(
        "bhe,khe->bhk", grad_ctx, values_all, preferred_element_type=jnp.float32
    )
    weighted = jnp.sum(probs * grad_probs, axis=-1, keepdims=True)
    grad_scores = (probs * (grad_probs - weighted)).astype(jnp.bfloat16)
    grad_q = (
        jnp.einsum("bhk,khe->bhe", grad_scores, keys_all, preferred_element_type=jnp.float32)
        * score_scale
    )
    grad_k = (
        jnp.einsum("bhk,bhe->khe", grad_scores, queries, preferred_element_type=jnp.float32)
        * score_scale
    )
    grad_v = jnp.einsum("bhk,bhe->khe", probs_low, grad_ctx, preferred_element_type=jnp.float32)
    return (context, grad_q, grad_k, grad_v)


def attention_kernel(
    q_ref, k_ref, v_ref, do_ref, st_ref, ctx_ref, dq_ref, dk_ref, dv_ref, *, tq, window, shift, scale
):
    qi = pl.program_id(1)
    a = pl.multiple_of(qi * tq, tq)

    @pl.when(qi == 0)
    def _():
        dk_ref[...] = jnp.zeros_like(dk_ref)
        dv_ref[...] = jnp.zeros_like(dv_ref)

    q = q_ref[...]
    k = k_ref[pl.ds(a, window), :]
    v = v_ref[pl.ds(a, window), :]
    do = do_ref[...]
    rows_t = (((1,), (1,)), ((), ()))
    cols_t = (((0,), (0,)), ((), ()))
    s = lax.dot_general(q, k, rows_t, preferred_element_type=jnp.float32) * scale
    key_idx = a + lax.broadcasted_iota(jnp.int32, (tq, window), 1)
    row_idx = a + shift + lax.broadcasted_iota(jnp.int32, (tq, window), 0)
    allowed = (key_idx >= st_ref[...]) & (key_idx <= row_idx)
    s = jnp.where(allowed, s, neg_large)
    row_top = jnp.max(s, axis=1, keepdims=True)
    log_total = row_top + jnp.log(jnp.sum(jnp.exp(s - row_top), axis=1, keepdims=True))
    p = jnp.exp(s - log_total)
    p_low = p.astype(jnp.bfloat16)
    ctx_ref[...] = jnp.dot(p_low, v, preferred_element_type=jnp.float32).astype(ctx_ref.dtype)
    dp = lax.dot_general(do, v, rows_t, preferred_element_type=jnp.float32)
    weighted = jnp.sum(p * dp, axis=1, keepdims=True)
    ds = (p * (dp - weighted)).astype(jnp.bfloat16)
    dq_ref[...] = (jnp.dot(ds, k, preferred_element_type=jnp.float32) * scale).astype(dq_ref.dtype)
    dk_ref[pl.ds(a, window), :] += lax.dot_general(ds, q, cols_t, preferred_element_type=jnp.float32)
    dv_ref[pl.ds(a, window), :] += lax.dot_general(p_low, do, cols_t, preferred_element_type=jnp.float32)


def attention(queries, keys_all, values_all, grad_ctx, rel_start):
    rows, width = queries.shape
    heads = width // HD
    tq = 256
    window = rows + tq
    kernel = functools.partial(
        attention_kernel, tq=tq, window=window, shift=rows, scale=HD ** (-0.5)
    )
    q_spec = pl.BlockSpec((tq, HD), lambda h, i: (i, h))
    kv_spec = pl.BlockSpec((2 * rows, HD), lambda h, i: (0, h))
    steps = heads * (rows // tq)
    cost = pl.CostEstimate(
        flops=steps * 12 * tq * window * HD,
        transcendentals=steps * 2 * tq * window,
        bytes_accessed=rows * width * 2 * 4 + 2 * rows * width * (2 * 2 + 4 * 2),
    )
    return pl.pallas_call(
        kernel,
        grid=(heads, rows // tq),
        in_specs=[q_spec, kv_spec, kv_spec, q_spec, pl.BlockSpec((tq, 1), lambda h, i: (i, 0))],
        out_specs=[q_spec, q_spec, kv_spec, kv_spec],
        out_shape=[
            jax.ShapeDtypeStruct((rows, width), jnp.bfloat16),
            jax.ShapeDtypeStruct((rows, width), jnp.bfloat16),
            jax.ShapeDtypeStruct((2 * rows, width), jnp.float32),
            jax.ShapeDtypeStruct((2 * rows, width), jnp.float32),
        ],
        compiler_params=pltpu.CompilerParams(dimension_semantics=("arbitrary", "arbitrary")),
        cost_estimate=cost,
    )(queries, keys_all, values_all, grad_ctx, rel_start)


def body(
    own_rows, gain, w_query, w_key, w_value, grad_context, send_slot, recv_slot, episode_start
):
    seq_count = lax.axis_size("seq")
    head_count = lax.axis_size("head")
    shard = lax.axis_index("seq")
    head_pos = lax.axis_index("head")
    row_count = own_rows.shape[0]
    capacity = 2 * row_count // seq_count
    width = own_rows.shape[1] // head_count
    own_part = lax.dynamic_slice_in_dim(own_rows, head_pos * width, width, 1)
    outgoing = (
        jnp.zeros((seq_count * capacity, width), own_rows.dtype)
        .at[send_slot]
        .set(own_part)
    )
    arrived = lax.all_to_all(outgoing, "seq", split_axis=0, concat_axis=0, tiled=True)
    packed_part = jnp.take(arrived, recv_slot, axis=0)
    packed = lax.all_gather(packed_part, "head", axis=1, tiled=True)
    rows_float = packed.astype(jnp.float32)
    inv_rms = lax.rsqrt(jnp.mean(rows_float * rows_float, axis=-1, keepdims=True) + epsilon)
    normed = (rows_float * inv_rms * gain).astype(jnp.bfloat16)
    queries = jnp.dot(normed, w_query, preferred_element_type=jnp.float32).astype(jnp.bfloat16)
    keys_own = jnp.dot(normed, w_key, preferred_element_type=jnp.float32).astype(jnp.bfloat16)
    values_own = jnp.dot(normed, w_value, preferred_element_type=jnp.float32).astype(jnp.bfloat16)
    rel_start = (episode_start - (shard - 1) * row_count).reshape(row_count, 1)
    local_heads = queries.shape[1] // HD
    outs = []
    for h in range(local_heads):
        cols = slice(h * HD, (h + 1) * HD)
        keys_h, values_h = keys_own[:, cols], values_own[:, cols]
        keys_prev, values_prev = passed_along((keys_h, values_h), "seq", 1)
        context_h, grad_q_h, grad_k_h, grad_v_h = attention(
            queries[:, cols],
            jnp.concatenate([keys_prev, keys_h], axis=0),
            jnp.concatenate([values_prev, values_h], axis=0),
            grad_context[:, cols],
            rel_start,
        )
        grad_k_h = grad_k_h * HD ** (-0.5)
        next_k, next_v = passed_along(
            (grad_k_h[:row_count].astype(jnp.bfloat16), grad_v_h[:row_count].astype(jnp.bfloat16)),
            "seq",
            -1,
        )
        grad_k_h = (grad_k_h[row_count:] + next_k.astype(jnp.float32)).astype(jnp.bfloat16)
        grad_v_h = (grad_v_h[row_count:] + next_v.astype(jnp.float32)).astype(jnp.bfloat16)
        outs.append((context_h, grad_q_h, grad_k_h, grad_v_h))
    context_out, grad_q_all, grad_k_all, grad_v_all = (
        jnp.concatenate(parts, axis=1) for parts in zip(*outs)
    )
    share = row_count // head_count

    def project(grads, weight):
        return jnp.einsum("rc,dc->rd", grads, weight, preferred_element_type=jnp.float32)

    grad_normed = lax.psum_scatter(
        (
            project(grad_q_all, w_query) + project(grad_k_all, w_key) + project(grad_v_all, w_value)
        ).astype(jnp.bfloat16),
        "head",
        scatter_dimension=0,
        tiled=True,
    ).astype(jnp.float32)
    own_start = head_pos * share
    mine = lax.dynamic_slice_in_dim(rows_float, own_start, share, 0)
    mine_inv = lax.dynamic_slice_in_dim(inv_rms, own_start, share, 0)
    gain_grad = gain * grad_normed
    mixed = jnp.mean(gain_grad * mine, axis=-1, keepdims=True)
    d_rows = (mine_inv * gain_grad - mine * mine_inv**3 * mixed).astype(jnp.bfloat16)
    return (context_out, d_rows)


def solution(mesh):
    in_specs = (
        P("seq", None),
        P(),
        P(None, "head"),
        P(None, "head"),
        P(None, "head"),
        P("seq", "head"),
        P("seq"),
        P("seq"),
        P("seq"),
    )
    out_specs = (P("seq", "head"), P(("seq", "head"), None))
    return jax.shard_map(body, mesh=mesh, in_specs=in_specs, out_specs=out_specs, check_vma=False)
```

```python
import functools

import jax
import jax.numpy as jnp
from jax import lax
from jax.experimental import pallas as pl
from jax.experimental.pallas import tpu as pltpu
from jax.sharding import PartitionSpec as P

HD = 128


neg_large = -1e30
epsilon = 1e-05


def passed_along(array, axis, by):
    count = lax.axis_size(axis)
    pairs = [(i, i + by) for i in range(count) if 0 <= i + by < count]
    return lax.ppermute(array, axis, pairs)


def block_terms(queries, keys_all, values_all, grad_ctx, starts, first_query, first_key):
    score_scale = queries.shape[-1] ** (-0.5)
    query_pos = first_query + jnp.arange(queries.shape[0], dtype=jnp.int32)
    key_pos = first_key + jnp.arange(keys_all.shape[0], dtype=jnp.int32)
    allowed = (key_pos[None, :] >= starts[:, None]) & (key_pos[None, :] <= query_pos[:, None])
    scores = (
        jnp.einsum("bhe,khe->bhk", queries, keys_all, preferred_element_type=jnp.float32)
        * score_scale
    )
    scores = jnp.where(allowed[:, None, :], scores, neg_large)
    row_top = jnp.max(scores, axis=-1, keepdims=True)
    log_total = row_top + jnp.log(jnp.sum(jnp.exp(scores - row_top), axis=-1, keepdims=True))
    probs = jnp.exp(scores - log_total)
    probs_low = probs.astype(jnp.bfloat16)
    context = jnp.einsum("bhk,khe->bhe", probs_low, values_all, preferred_element_type=jnp.float32)
    grad_probs = jnp.einsum(
        "bhe,khe->bhk", grad_ctx, values_all, preferred_element_type=jnp.float32
    )
    weighted = jnp.sum(probs * grad_probs, axis=-1, keepdims=True)
    grad_scores = (probs * (grad_probs - weighted)).astype(jnp.bfloat16)
    grad_q = (
        jnp.einsum("bhk,khe->bhe", grad_scores, keys_all, preferred_element_type=jnp.float32)
        * score_scale
    )
    grad_k = (
        jnp.einsum("bhk,bhe->khe", grad_scores, queries, preferred_element_type=jnp.float32)
        * score_scale
    )
    grad_v = jnp.einsum("bhk,bhe->khe", probs_low, grad_ctx, preferred_element_type=jnp.float32)
    return (context, grad_q, grad_k, grad_v)


def attention_kernel(
    q_ref, kp_ref, vp_ref, ko_ref, vo_ref, do_ref, st_ref,
    ctx_ref, dq_ref, send_ref, keep_ref,
    k_scr, v_scr, dk_scr, dv_scr, *, tq, window, shift, scale
):
    qi = pl.program_id(0)
    a = pl.multiple_of(qi * tq, tq)
    half = kp_ref.shape[0]

    @pl.when(qi == 0)
    def _():
        k_scr[:half, :] = kp_ref[...]
        k_scr[half:, :] = ko_ref[...]
        v_scr[:half, :] = vp_ref[...]
        v_scr[half:, :] = vo_ref[...]
        dk_scr[...] = jnp.zeros_like(dk_scr)
        dv_scr[...] = jnp.zeros_like(dv_scr)

    q = q_ref[...]
    k = k_scr[pl.ds(a, window), :]
    v = v_scr[pl.ds(a, window), :]
    do = do_ref[...]
    rows_t = (((1,), (1,)), ((), ()))
    cols_t = (((0,), (0,)), ((), ()))
    s = lax.dot_general(q, k, rows_t, preferred_element_type=jnp.float32) * scale
    key_idx = a + lax.broadcasted_iota(jnp.int32, (tq, window), 1)
    row_idx = a + shift + lax.broadcasted_iota(jnp.int32, (tq, window), 0)
    allowed = (key_idx >= st_ref[...]) & (key_idx <= row_idx)
    s = jnp.where(allowed, s, neg_large)
    row_top = jnp.max(s, axis=1, keepdims=True)
    log_total = row_top + jnp.log(jnp.sum(jnp.exp(s - row_top), axis=1, keepdims=True))
    p = jnp.exp(s - log_total)
    p_low = p.astype(jnp.bfloat16)
    ctx_ref[...] = jnp.dot(p_low, v, preferred_element_type=jnp.float32).astype(ctx_ref.dtype)
    dp = lax.dot_general(do, v, rows_t, preferred_element_type=jnp.float32)
    weighted = jnp.sum(p * dp, axis=1, keepdims=True)
    ds = (p * (dp - weighted)).astype(jnp.bfloat16)
    dq_ref[...] = (jnp.dot(ds, k, preferred_element_type=jnp.float32) * scale).astype(dq_ref.dtype)
    dk_scr[pl.ds(a, window), :] += lax.dot_general(ds, q, cols_t, preferred_element_type=jnp.float32)
    dv_scr[pl.ds(a, window), :] += lax.dot_general(p_low, do, cols_t, preferred_element_type=jnp.float32)

    @pl.when(qi == pl.num_programs(0) - 1)
    def _():
        hd = q_ref.shape[1]
        send_ref[:, :hd] = (dk_scr[:half, :] * scale).astype(send_ref.dtype)
        send_ref[:, hd:] = dv_scr[:half, :].astype(send_ref.dtype)
        keep_ref[:, :hd] = dk_scr[half:, :] * scale
        keep_ref[:, hd:] = dv_scr[half:, :]


def attention(queries, kv_prev, kv_own, grad_ctx, rel_start):
    rows, hd = queries.shape
    tq = 256
    window = rows + tq
    kernel = functools.partial(
        attention_kernel, tq=tq, window=window, shift=rows, scale=hd ** (-0.5)
    )
    q_spec = pl.BlockSpec((tq, hd), lambda i: (i, 0))
    k_spec = pl.BlockSpec((rows, hd), lambda i: (0, 0))
    v_spec = pl.BlockSpec((rows, hd), lambda i: (0, 1))
    kv_spec = pl.BlockSpec((rows, 2 * hd), lambda i: (0, 0))
    steps = rows // tq
    cost = pl.CostEstimate(
        flops=steps * 12 * tq * window * hd,
        transcendentals=steps * 2 * tq * window,
        bytes_accessed=rows * hd * 2 * 8 + rows * 2 * hd * 6,
    )
    return pl.pallas_call(
        kernel,
        grid=(steps,),
        in_specs=[q_spec, k_spec, v_spec, k_spec, v_spec, q_spec,
                  pl.BlockSpec((tq, 1), lambda i: (i, 0))],
        out_specs=[q_spec, q_spec, kv_spec, kv_spec],
        out_shape=[
            jax.ShapeDtypeStruct((rows, hd), jnp.bfloat16),
            jax.ShapeDtypeStruct((rows, hd), jnp.bfloat16),
            jax.ShapeDtypeStruct((rows, 2 * hd), jnp.bfloat16),
            jax.ShapeDtypeStruct((rows, 2 * hd), jnp.float32),
        ],
        scratch_shapes=[pltpu.VMEM((2 * rows, hd), jnp.bfloat16)] * 2
        + [pltpu.VMEM((2 * rows, hd), jnp.float32)] * 2,
        compiler_params=pltpu.CompilerParams(dimension_semantics=("arbitrary",)),
        cost_estimate=cost,
    )(queries, kv_prev, kv_prev, kv_own, kv_own, grad_ctx, rel_start)


def body(
    own_rows, gain, w_query, w_key, w_value, grad_context, send_slot, recv_slot, episode_start
):
    seq_count = lax.axis_size("seq")
    head_count = lax.axis_size("head")
    shard = lax.axis_index("seq")
    head_pos = lax.axis_index("head")
    row_count = own_rows.shape[0]
    capacity = 2 * row_count // seq_count
    width = own_rows.shape[1] // head_count
    own_part = lax.dynamic_slice_in_dim(own_rows, head_pos * width, width, 1)
    outgoing = (
        jnp.zeros((seq_count * capacity, width), own_rows.dtype)
        .at[send_slot]
        .set(own_part)
    )
    arrived = lax.all_to_all(outgoing, "seq", split_axis=0, concat_axis=0, tiled=True)
    packed_part = jnp.take(arrived, recv_slot, axis=0)
    packed = lax.all_gather(packed_part, "head", axis=1, tiled=True)
    rows_float = packed.astype(jnp.float32)
    inv_rms = lax.rsqrt(jnp.mean(rows_float * rows_float, axis=-1, keepdims=True) + epsilon)
    normed = (rows_float * inv_rms * gain).astype(jnp.bfloat16)
    queries = jnp.dot(normed, w_query, preferred_element_type=jnp.float32).astype(jnp.bfloat16)
    rel_start = (episode_start - (shard - 1) * row_count).reshape(row_count, 1)
    local_heads = queries.shape[1] // HD
    contexts, grad_queries, kv_parts = [], [], []
    for h in range(local_heads):
        cols = slice(h * HD, (h + 1) * HD)
        kv_weight = jnp.concatenate([w_key[:, cols], w_value[:, cols]], axis=1)
        kv_own = jnp.dot(normed, kv_weight, preferred_element_type=jnp.float32).astype(jnp.bfloat16)
        kv_prev = passed_along(kv_own, "seq", 1)
        context_h, grad_q_h, kv_send, kv_keep = attention(
            queries[:, cols], kv_prev, kv_own, grad_context[:, cols], rel_start
        )
        kv_next = passed_along(kv_send, "seq", -1)
        grad_kv = (kv_keep + kv_next.astype(jnp.float32)).astype(jnp.bfloat16)
        contexts.append(context_h)
        grad_queries.append(grad_q_h)
        kv_parts.append((grad_kv, kv_weight))
    context_out = jnp.concatenate(contexts, axis=1)
    grad_q_all = jnp.concatenate(grad_queries, axis=1)
    share = row_count // head_count

    def project(grads, weight):
        return jnp.einsum("rc,dc->rd", grads, weight, preferred_element_type=jnp.float32)

    term = project(grad_q_all, w_query)
    for grad_kv, kv_weight in kv_parts:
        term = term + project(grad_kv, kv_weight)
    grad_normed = lax.psum_scatter(
        term.astype(jnp.bfloat16),
        "head",
        scatter_dimension=0,
        tiled=True,
    ).astype(jnp.float32)
    own_start = head_pos * share
    mine = lax.dynamic_slice_in_dim(packed, own_start, share, 0).astype(jnp.float32)
    mine_inv = lax.dynamic_slice_in_dim(inv_rms, own_start, share, 0)
    gain_grad = gain * grad_normed
    mixed = jnp.mean(gain_grad * mine, axis=-1, keepdims=True)
    d_rows = (mine_inv * gain_grad - mine * mine_inv**3 * mixed).astype(jnp.bfloat16)
    return (context_out, d_rows)


def solution(mesh):
    in_specs = (
        P("seq", None),
        P(),
        P(None, "head"),
        P(None, "head"),
        P(None, "head"),
        P("seq", "head"),
        P("seq"),
        P("seq"),
        P("seq"),
    )
    out_specs = (P("seq", "head"), P(("seq", "head"), None))
    return jax.shard_map(body, mesh=mesh, in_specs=in_specs, out_specs=out_specs, check_vma=False)
```

```python
import functools

import jax
import jax.numpy as jnp
from jax import lax
from jax.experimental import pallas as pl
from jax.experimental.pallas import tpu as pltpu
from jax.sharding import PartitionSpec as P

HD = 128


neg_large = -1e30
epsilon = 1e-05


def passed_along(array, axis, by):
    count = lax.axis_size(axis)
    pairs = [(i, i + by) for i in range(count) if 0 <= i + by < count]
    return lax.ppermute(array, axis, pairs)


def block_terms(queries, keys_all, values_all, grad_ctx, starts, first_query, first_key):
    score_scale = queries.shape[-1] ** (-0.5)
    query_pos = first_query + jnp.arange(queries.shape[0], dtype=jnp.int32)
    key_pos = first_key + jnp.arange(keys_all.shape[0], dtype=jnp.int32)
    allowed = (key_pos[None, :] >= starts[:, None]) & (key_pos[None, :] <= query_pos[:, None])
    scores = (
        jnp.einsum("bhe,khe->bhk", queries, keys_all, preferred_element_type=jnp.float32)
        * score_scale
    )
    scores = jnp.where(allowed[:, None, :], scores, neg_large)
    row_top = jnp.max(scores, axis=-1, keepdims=True)
    log_total = row_top + jnp.log(jnp.sum(jnp.exp(scores - row_top), axis=-1, keepdims=True))
    probs = jnp.exp(scores - log_total)
    probs_low = probs.astype(jnp.bfloat16)
    context = jnp.einsum("bhk,khe->bhe", probs_low, values_all, preferred_element_type=jnp.float32)
    grad_probs = jnp.einsum(
        "bhe,khe->bhk", grad_ctx, values_all, preferred_element_type=jnp.float32
    )
    weighted = jnp.sum(probs * grad_probs, axis=-1, keepdims=True)
    grad_scores = (probs * (grad_probs - weighted)).astype(jnp.bfloat16)
    grad_q = (
        jnp.einsum("bhk,khe->bhe", grad_scores, keys_all, preferred_element_type=jnp.float32)
        * score_scale
    )
    grad_k = (
        jnp.einsum("bhk,bhe->khe", grad_scores, queries, preferred_element_type=jnp.float32)
        * score_scale
    )
    grad_v = jnp.einsum("bhk,bhe->khe", probs_low, grad_ctx, preferred_element_type=jnp.float32)
    return (context, grad_q, grad_k, grad_v)


def attention_kernel(*refs, pieces, tq, window, shift, scale):
    q_ref = refs[0]
    kv_refs = refs[1 : 1 + 4 * pieces]
    do_ref, st_ref, ctx_ref, dq_ref, send_ref, keep_ref, k_scr, v_scr, dk_scr, dv_scr = refs[
        1 + 4 * pieces :
    ]
    qi = pl.program_id(0)
    a = pl.multiple_of(qi * tq, tq)
    piece = kv_refs[0].shape[0]
    half = piece * pieces

    @pl.when(qi == 0)
    def _():
        for j in range(2 * pieces):
            k_scr[j * piece : (j + 1) * piece, :] = kv_refs[2 * j][...]
            v_scr[j * piece : (j + 1) * piece, :] = kv_refs[2 * j + 1][...]
        dk_scr[...] = jnp.zeros_like(dk_scr)
        dv_scr[...] = jnp.zeros_like(dv_scr)

    q = q_ref[...]
    k = k_scr[pl.ds(a, window), :]
    v = v_scr[pl.ds(a, window), :]
    do = do_ref[...]
    rows_t = (((1,), (1,)), ((), ()))
    cols_t = (((0,), (0,)), ((), ()))
    s = lax.dot_general(q, k, rows_t, preferred_element_type=jnp.float32) * scale
    key_idx = a + lax.broadcasted_iota(jnp.int32, (tq, window), 1)
    row_idx = a + shift + lax.broadcasted_iota(jnp.int32, (tq, window), 0)
    allowed = (key_idx >= st_ref[...]) & (key_idx <= row_idx)
    s = jnp.where(allowed, s, neg_large)
    row_top = jnp.max(s, axis=1, keepdims=True)
    log_total = row_top + jnp.log(jnp.sum(jnp.exp(s - row_top), axis=1, keepdims=True))
    p = jnp.exp(s - log_total)
    p_low = p.astype(jnp.bfloat16)
    ctx_ref[...] = jnp.dot(p_low, v, preferred_element_type=jnp.float32).astype(ctx_ref.dtype)
    dp = lax.dot_general(do, v, rows_t, preferred_element_type=jnp.float32)
    weighted = jnp.sum(p * dp, axis=1, keepdims=True)
    ds = (p * (dp - weighted)).astype(jnp.bfloat16)
    dq_ref[...] = (jnp.dot(ds, k, preferred_element_type=jnp.float32) * scale).astype(dq_ref.dtype)
    dk_scr[pl.ds(a, window), :] += lax.dot_general(ds, q, cols_t, preferred_element_type=jnp.float32)
    dv_scr[pl.ds(a, window), :] += lax.dot_general(p_low, do, cols_t, preferred_element_type=jnp.float32)

    @pl.when(qi == pl.num_programs(0) - 1)
    def _():
        hd = q_ref.shape[1]
        send_ref[:, :hd] = (dk_scr[:half, :] * scale).astype(send_ref.dtype)
        send_ref[:, hd:] = dv_scr[:half, :].astype(send_ref.dtype)
        keep_ref[:, :hd] = dk_scr[half:, :] * scale
        keep_ref[:, hd:] = dv_scr[half:, :]


def attention(queries, kv_prev, kv_own, grad_ctx, rel_start):
    rows, hd = queries.shape
    pieces = len(kv_prev)
    piece = rows // pieces
    tq = 256
    window = rows + tq
    kernel = functools.partial(
        attention_kernel, pieces=pieces, tq=tq, window=window, shift=rows, scale=hd ** (-0.5)
    )
    q_spec = pl.BlockSpec((tq, hd), lambda i: (i, 0))
    k_spec = pl.BlockSpec((piece, hd), lambda i: (0, 0))
    v_spec = pl.BlockSpec((piece, hd), lambda i: (0, 1))
    kv_spec = pl.BlockSpec((rows, 2 * hd), lambda i: (0, 0))
    steps = rows // tq
    cost = pl.CostEstimate(
        flops=steps * 12 * tq * window * hd,
        transcendentals=steps * 2 * tq * window,
        bytes_accessed=rows * hd * 2 * 8 + rows * 2 * hd * 6,
    )
    kv_args = []
    for part in list(kv_prev) + list(kv_own):
        kv_args += [part, part]
    return pl.pallas_call(
        kernel,
        grid=(steps,),
        in_specs=[q_spec] + [k_spec, v_spec] * (2 * pieces) + [
            q_spec, pl.BlockSpec((tq, 1), lambda i: (i, 0))],
        out_specs=[q_spec, q_spec, kv_spec, kv_spec],
        out_shape=[
            jax.ShapeDtypeStruct((rows, hd), jnp.bfloat16),
            jax.ShapeDtypeStruct((rows, hd), jnp.bfloat16),
            jax.ShapeDtypeStruct((rows, 2 * hd), jnp.bfloat16),
            jax.ShapeDtypeStruct((rows, 2 * hd), jnp.float32),
        ],
        scratch_shapes=[pltpu.VMEM((2 * rows, hd), jnp.bfloat16)] * 2
        + [pltpu.VMEM((2 * rows, hd), jnp.float32)] * 2,
        compiler_params=pltpu.CompilerParams(dimension_semantics=("arbitrary",)),
        cost_estimate=cost,
    )(queries, *kv_args, grad_ctx, rel_start)


def body(
    own_rows, gain, w_query, w_key, w_value, grad_context, send_slot, recv_slot, episode_start
):
    seq_count = lax.axis_size("seq")
    head_count = lax.axis_size("head")
    shard = lax.axis_index("seq")
    head_pos = lax.axis_index("head")
    row_count = own_rows.shape[0]
    capacity = 2 * row_count // seq_count
    width = own_rows.shape[1] // head_count
    own_part = lax.dynamic_slice_in_dim(own_rows, head_pos * width, width, 1)
    outgoing = (
        jnp.zeros((seq_count * capacity, width), own_rows.dtype)
        .at[send_slot]
        .set(own_part)
    )
    arrived = lax.all_to_all(outgoing, "seq", split_axis=0, concat_axis=0, tiled=True)
    packed_part = jnp.take(arrived, recv_slot, axis=0)
    pieces = 2
    piece = row_count // pieces
    rel_start = (episode_start - (shard - 1) * row_count).reshape(row_count, 1)
    local_heads = w_query.shape[1] // HD
    kv_weights = [
        jnp.concatenate([w_key[:, h * HD : (h + 1) * HD], w_value[:, h * HD : (h + 1) * HD]], axis=1)
        for h in range(local_heads)
    ]
    packed_pieces, inv_pieces, query_pieces = [], [], []
    kv_own = [[] for _ in range(local_heads)]
    kv_prev = [[] for _ in range(local_heads)]
    for c in range(pieces):
        part_c = packed_part[c * piece : (c + 1) * piece]
        if c > 0:
            part_c, _ = lax.optimization_barrier((part_c, [kv[-1] for kv in kv_own]))
        packed_c = lax.all_gather(part_c, "head", axis=1, tiled=True)
        rows_float = packed_c.astype(jnp.float32)
        inv_rms = lax.rsqrt(jnp.mean(rows_float * rows_float, axis=-1, keepdims=True) + epsilon)
        normed = (rows_float * inv_rms * gain).astype(jnp.bfloat16)
        query_pieces.append(
            jnp.dot(normed, w_query, preferred_element_type=jnp.float32).astype(jnp.bfloat16)
        )
        for h in range(local_heads):
            kv_c = jnp.dot(normed, kv_weights[h], preferred_element_type=jnp.float32).astype(
                jnp.bfloat16
            )
            kv_own[h].append(kv_c)
            kv_prev[h].append(passed_along(kv_c, "seq", 1))
        packed_pieces.append(packed_c)
        inv_pieces.append(inv_rms)
    queries = jnp.concatenate(query_pieces, axis=0)
    contexts, grad_queries, kv_parts = [], [], []
    for h in range(local_heads):
        cols = slice(h * HD, (h + 1) * HD)
        context_h, grad_q_h, kv_send, kv_keep = attention(
            queries[:, cols], kv_prev[h], kv_own[h], grad_context[:, cols], rel_start
        )
        kv_next = passed_along(kv_send, "seq", -1)
        grad_kv = (kv_keep + kv_next.astype(jnp.float32)).astype(jnp.bfloat16)
        contexts.append(context_h)
        grad_queries.append(grad_q_h)
        kv_parts.append((grad_kv, kv_weights[h]))
    context_out = jnp.concatenate(contexts, axis=1)
    grad_q_all = jnp.concatenate(grad_queries, axis=1)
    share = row_count // head_count

    def project(grads, weight):
        return jnp.einsum("rc,dc->rd", grads, weight, preferred_element_type=jnp.float32)

    term = project(grad_q_all, w_query)
    for grad_kv, kv_weight in kv_parts:
        term = term + project(grad_kv, kv_weight)
    grad_normed = lax.psum_scatter(
        term.astype(jnp.bfloat16),
        "head",
        scatter_dimension=0,
        tiled=True,
    ).astype(jnp.float32)
    per_piece = piece // share
    local_start = (head_pos % per_piece) * share
    mine = lax.dynamic_slice_in_dim(packed_pieces[0], local_start, share, 0)
    mine_inv = lax.dynamic_slice_in_dim(inv_pieces[0], local_start, share, 0)
    for c in range(1, pieces):
        later = head_pos // per_piece == c
        mine = jnp.where(later, lax.dynamic_slice_in_dim(packed_pieces[c], local_start, share, 0), mine)
        mine_inv = jnp.where(
            later, lax.dynamic_slice_in_dim(inv_pieces[c], local_start, share, 0), mine_inv
        )
    mine = mine.astype(jnp.float32)
    gain_grad = gain * grad_normed
    mixed = jnp.mean(gain_grad * mine, axis=-1, keepdims=True)
    d_rows = (mine_inv * gain_grad - mine * mine_inv**3 * mixed).astype(jnp.bfloat16)
    return (context_out, d_rows)


def solution(mesh):
    in_specs = (
        P("seq", None),
        P(),
        P(None, "head"),
        P(None, "head"),
        P(None, "head"),
        P("seq", "head"),
        P("seq"),
        P("seq"),
        P("seq"),
    )
    out_specs = (P("seq", "head"), P(("seq", "head"), None))
    return jax.shard_map(body, mesh=mesh, in_specs=in_specs, out_specs=out_specs, check_vma=False)
```

```python
import functools

import jax
import jax.numpy as jnp
from jax import lax
from jax.experimental import pallas as pl
from jax.experimental.pallas import tpu as pltpu
from jax.sharding import PartitionSpec as P

HD = 128


neg_large = -1e30
epsilon = 1e-05


def passed_along(array, axis, by):
    count = lax.axis_size(axis)
    pairs = [(i, i + by) for i in range(count) if 0 <= i + by < count]
    return lax.ppermute(array, axis, pairs)


def block_terms(queries, keys_all, values_all, grad_ctx, starts, first_query, first_key):
    score_scale = queries.shape[-1] ** (-0.5)
    query_pos = first_query + jnp.arange(queries.shape[0], dtype=jnp.int32)
    key_pos = first_key + jnp.arange(keys_all.shape[0], dtype=jnp.int32)
    allowed = (key_pos[None, :] >= starts[:, None]) & (key_pos[None, :] <= query_pos[:, None])
    scores = (
        jnp.einsum("bhe,khe->bhk", queries, keys_all, preferred_element_type=jnp.float32)
        * score_scale
    )
    scores = jnp.where(allowed[:, None, :], scores, neg_large)
    row_top = jnp.max(scores, axis=-1, keepdims=True)
    log_total = row_top + jnp.log(jnp.sum(jnp.exp(scores - row_top), axis=-1, keepdims=True))
    probs = jnp.exp(scores - log_total)
    probs_low = probs.astype(jnp.bfloat16)
    context = jnp.einsum("bhk,khe->bhe", probs_low, values_all, preferred_element_type=jnp.float32)
    grad_probs = jnp.einsum(
        "bhe,khe->bhk", grad_ctx, values_all, preferred_element_type=jnp.float32
    )
    weighted = jnp.sum(probs * grad_probs, axis=-1, keepdims=True)
    grad_scores = (probs * (grad_probs - weighted)).astype(jnp.bfloat16)
    grad_q = (
        jnp.einsum("bhk,khe->bhe", grad_scores, keys_all, preferred_element_type=jnp.float32)
        * score_scale
    )
    grad_k = (
        jnp.einsum("bhk,bhe->khe", grad_scores, queries, preferred_element_type=jnp.float32)
        * score_scale
    )
    grad_v = jnp.einsum("bhk,bhe->khe", probs_low, grad_ctx, preferred_element_type=jnp.float32)
    return (context, grad_q, grad_k, grad_v)


def attention_kernel(
    q_ref, kp_ref, vp_ref, ko_ref, vo_ref, do_ref, st_ref,
    ctx_ref, dq_ref, send_ref, keep_ref,
    k_scr, v_scr, dk_scr, dv_scr, *, tq, window, shift, scale
):
    qi = pl.program_id(0)
    a = pl.multiple_of(qi * tq, tq)
    half = kp_ref.shape[0]

    @pl.when(qi == 0)
    def _():
        k_scr[:half, :] = kp_ref[...]
        k_scr[half:, :] = ko_ref[...]
        v_scr[:half, :] = vp_ref[...]
        v_scr[half:, :] = vo_ref[...]
        dk_scr[...] = jnp.zeros_like(dk_scr)
        dv_scr[...] = jnp.zeros_like(dv_scr)

    q = q_ref[...]
    k = k_scr[pl.ds(a, window), :]
    v = v_scr[pl.ds(a, window), :]
    do = do_ref[...]
    rows_t = (((1,), (1,)), ((), ()))
    cols_t = (((0,), (0,)), ((), ()))
    s = lax.dot_general(q, k, rows_t, preferred_element_type=jnp.float32) * scale
    key_idx = a + lax.broadcasted_iota(jnp.int32, (tq, window), 1)
    row_idx = a + shift + lax.broadcasted_iota(jnp.int32, (tq, window), 0)
    allowed = (key_idx >= st_ref[...]) & (key_idx <= row_idx)
    s = jnp.where(allowed, s, neg_large)
    row_top = jnp.max(s, axis=1, keepdims=True)
    log_total = row_top + jnp.log(jnp.sum(jnp.exp(s - row_top), axis=1, keepdims=True))
    p = jnp.exp(s - log_total)
    p_low = p.astype(jnp.bfloat16)
    ctx_ref[...] = jnp.dot(p_low, v, preferred_element_type=jnp.float32).astype(ctx_ref.dtype)
    dp = lax.dot_general(do, v, rows_t, preferred_element_type=jnp.float32)
    weighted = jnp.sum(p * dp, axis=1, keepdims=True)
    ds = (p * (dp - weighted)).astype(jnp.bfloat16)
    dq_ref[...] = (jnp.dot(ds, k, preferred_element_type=jnp.float32) * scale).astype(dq_ref.dtype)
    dk_scr[pl.ds(a, window), :] += lax.dot_general(ds, q, cols_t, preferred_element_type=jnp.float32)
    dv_scr[pl.ds(a, window), :] += lax.dot_general(p_low, do, cols_t, preferred_element_type=jnp.float32)

    @pl.when(qi == pl.num_programs(0) - 1)
    def _():
        hd = q_ref.shape[1]
        send_ref[:, :hd] = (dk_scr[:half, :] * scale).astype(send_ref.dtype)
        send_ref[:, hd:] = dv_scr[:half, :].astype(send_ref.dtype)
        keep_ref[:, :hd] = dk_scr[half:, :] * scale
        keep_ref[:, hd:] = dv_scr[half:, :]


def attention(queries, kv_prev, kv_own, grad_ctx, rel_start):
    rows, hd = queries.shape
    tq = 256
    window = rows + tq
    kernel = functools.partial(
        attention_kernel, tq=tq, window=window, shift=rows, scale=hd ** (-0.5)
    )
    q_spec = pl.BlockSpec((tq, hd), lambda i: (i, 0))
    k_spec = pl.BlockSpec((rows, hd), lambda i: (0, 0))
    v_spec = pl.BlockSpec((rows, hd), lambda i: (0, 1))
    kv_spec = pl.BlockSpec((rows, 2 * hd), lambda i: (0, 0))
    steps = rows // tq
    cost = pl.CostEstimate(
        flops=steps * 12 * tq * window * hd,
        transcendentals=steps * 2 * tq * window,
        bytes_accessed=rows * hd * 2 * 8 + rows * 2 * hd * 6,
    )
    return pl.pallas_call(
        kernel,
        grid=(steps,),
        in_specs=[q_spec, k_spec, v_spec, k_spec, v_spec, q_spec,
                  pl.BlockSpec((tq, 1), lambda i: (i, 0))],
        out_specs=[q_spec, q_spec, kv_spec, kv_spec],
        out_shape=[
            jax.ShapeDtypeStruct((rows, hd), jnp.bfloat16),
            jax.ShapeDtypeStruct((rows, hd), jnp.bfloat16),
            jax.ShapeDtypeStruct((rows, 2 * hd), jnp.bfloat16),
            jax.ShapeDtypeStruct((rows, 2 * hd), jnp.float32),
        ],
        scratch_shapes=[pltpu.VMEM((2 * rows, hd), jnp.bfloat16)] * 2
        + [pltpu.VMEM((2 * rows, hd), jnp.float32)] * 2,
        compiler_params=pltpu.CompilerParams(dimension_semantics=("arbitrary",)),
        cost_estimate=cost,
    )(queries, kv_prev, kv_prev, kv_own, kv_own, grad_ctx, rel_start)


def body(
    own_rows, gain, w_query, w_key, w_value, grad_context, send_slot, recv_slot, episode_start
):
    seq_count = lax.axis_size("seq")
    head_count = lax.axis_size("head")
    shard = lax.axis_index("seq")
    head_pos = lax.axis_index("head")
    row_count = own_rows.shape[0]
    capacity = 2 * row_count // seq_count
    width = own_rows.shape[1] // head_count
    own_part = lax.dynamic_slice_in_dim(own_rows, head_pos * width, width, 1)
    slots = seq_count * capacity
    send_pick = (
        lax.broadcasted_iota(jnp.int32, (slots, row_count), 0) == send_slot[None, :]
    ).astype(own_rows.dtype)
    outgoing = jnp.dot(send_pick, own_part, preferred_element_type=jnp.float32).astype(
        own_rows.dtype
    )
    arrived = lax.all_to_all(outgoing, "seq", split_axis=0, concat_axis=0, tiled=True)
    recv_pick = (
        lax.broadcasted_iota(jnp.int32, (row_count, slots), 1) == recv_slot[:, None]
    ).astype(own_rows.dtype)
    packed_part = jnp.dot(recv_pick, arrived, preferred_element_type=jnp.float32).astype(
        own_rows.dtype
    )
    packed = lax.all_gather(packed_part, "head", axis=1, tiled=True)
    rows_float = packed.astype(jnp.float32)
    inv_rms = lax.rsqrt(jnp.mean(rows_float * rows_float, axis=-1, keepdims=True) + epsilon)
    normed = (rows_float * inv_rms * gain).astype(jnp.bfloat16)
    queries = jnp.dot(normed, w_query, preferred_element_type=jnp.float32).astype(jnp.bfloat16)
    rel_start = (episode_start - (shard - 1) * row_count).reshape(row_count, 1)
    local_heads = queries.shape[1] // HD
    contexts, grad_queries, kv_parts = [], [], []
    for h in range(local_heads):
        cols = slice(h * HD, (h + 1) * HD)
        kv_weight = jnp.concatenate([w_key[:, cols], w_value[:, cols]], axis=1)
        kv_own = jnp.dot(normed, kv_weight, preferred_element_type=jnp.float32).astype(jnp.bfloat16)
        kv_prev = passed_along(kv_own, "seq", 1)
        context_h, grad_q_h, kv_send, kv_keep = attention(
            queries[:, cols], kv_prev, kv_own, grad_context[:, cols], rel_start
        )
        kv_next = passed_along(kv_send, "seq", -1)
        grad_kv = (kv_keep + kv_next.astype(jnp.float32)).astype(jnp.bfloat16)
        contexts.append(context_h)
        grad_queries.append(grad_q_h)
        kv_parts.append((grad_kv, kv_weight))
    context_out = jnp.concatenate(contexts, axis=1)
    grad_q_all = jnp.concatenate(grad_queries, axis=1)
    share = row_count // head_count

    def project(grads, weight):
        return jnp.einsum("rc,dc->rd", grads, weight, preferred_element_type=jnp.float32)

    term = project(grad_q_all, w_query)
    for grad_kv, kv_weight in kv_parts:
        term = term + project(grad_kv, kv_weight)
    grad_normed = lax.psum_scatter(
        term.astype(jnp.bfloat16),
        "head",
        scatter_dimension=0,
        tiled=True,
    ).astype(jnp.float32)
    own_start = head_pos * share
    mine = lax.dynamic_slice_in_dim(packed, own_start, share, 0).astype(jnp.float32)
    mine_inv = lax.dynamic_slice_in_dim(inv_rms, own_start, share, 0)
    gain_grad = gain * grad_normed
    mixed = jnp.mean(gain_grad * mine, axis=-1, keepdims=True)
    d_rows = (mine_inv * gain_grad - mine * mine_inv**3 * mixed).astype(jnp.bfloat16)
    return (context_out, d_rows)


def solution(mesh):
    in_specs = (
        P("seq", None),
        P(),
        P(None, "head"),
        P(None, "head"),
        P(None, "head"),
        P("seq", "head"),
        P("seq"),
        P("seq"),
        P("seq"),
    )
    out_specs = (P("seq", "head"), P(("seq", "head"), None))
    return jax.shard_map(body, mesh=mesh, in_specs=in_specs, out_specs=out_specs, check_vma=False)
```

```python
import functools

import jax
import jax.numpy as jnp
from jax import lax
from jax.experimental import pallas as pl
from jax.experimental.pallas import tpu as pltpu
from jax.sharding import PartitionSpec as P

HD = 128


neg_large = -1e30
epsilon = 1e-05


def passed_along(array, axis, by):
    count = lax.axis_size(axis)
    pairs = [(i, i + by) for i in range(count) if 0 <= i + by < count]
    return lax.ppermute(array, axis, pairs)


def block_terms(queries, keys_all, values_all, grad_ctx, starts, first_query, first_key):
    score_scale = queries.shape[-1] ** (-0.5)
    query_pos = first_query + jnp.arange(queries.shape[0], dtype=jnp.int32)
    key_pos = first_key + jnp.arange(keys_all.shape[0], dtype=jnp.int32)
    allowed = (key_pos[None, :] >= starts[:, None]) & (key_pos[None, :] <= query_pos[:, None])
    scores = (
        jnp.einsum("bhe,khe->bhk", queries, keys_all, preferred_element_type=jnp.float32)
        * score_scale
    )
    scores = jnp.where(allowed[:, None, :], scores, neg_large)
    row_top = jnp.max(scores, axis=-1, keepdims=True)
    log_total = row_top + jnp.log(jnp.sum(jnp.exp(scores - row_top), axis=-1, keepdims=True))
    probs = jnp.exp(scores - log_total)
    probs_low = probs.astype(jnp.bfloat16)
    context = jnp.einsum("bhk,khe->bhe", probs_low, values_all, preferred_element_type=jnp.float32)
    grad_probs = jnp.einsum(
        "bhe,khe->bhk", grad_ctx, values_all, preferred_element_type=jnp.float32
    )
    weighted = jnp.sum(probs * grad_probs, axis=-1, keepdims=True)
    grad_scores = (probs * (grad_probs - weighted)).astype(jnp.bfloat16)
    grad_q = (
        jnp.einsum("bhk,khe->bhe", grad_scores, keys_all, preferred_element_type=jnp.float32)
        * score_scale
    )
    grad_k = (
        jnp.einsum("bhk,bhe->khe", grad_scores, queries, preferred_element_type=jnp.float32)
        * score_scale
    )
    grad_v = jnp.einsum("bhk,bhe->khe", probs_low, grad_ctx, preferred_element_type=jnp.float32)
    return (context, grad_q, grad_k, grad_v)


def attention_kernel(
    q_ref, kp_ref, vp_ref, ko_ref, vo_ref, do_ref, st_ref,
    ctx_ref, dq_ref, send_ref, keep_ref,
    k_scr, v_scr, dk_scr, dv_scr, *, tq, window, shift, scale
):
    qi = pl.program_id(0)
    a = pl.multiple_of(qi * tq, tq)
    half = kp_ref.shape[0]

    @pl.when(qi == 0)
    def _():
        k_scr[:half, :] = kp_ref[...]
        k_scr[half:, :] = ko_ref[...]
        v_scr[:half, :] = vp_ref[...]
        v_scr[half:, :] = vo_ref[...]
        dk_scr[...] = jnp.zeros_like(dk_scr)
        dv_scr[...] = jnp.zeros_like(dv_scr)

    q = q_ref[...]
    k = k_scr[pl.ds(a, window), :]
    v = v_scr[pl.ds(a, window), :]
    do = do_ref[...]
    rows_t = (((1,), (1,)), ((), ()))
    cols_t = (((0,), (0,)), ((), ()))
    s = lax.dot_general(q, k, rows_t, preferred_element_type=jnp.float32) * scale
    key_idx = a + lax.broadcasted_iota(jnp.int32, (tq, window), 1)
    row_idx = a + shift + lax.broadcasted_iota(jnp.int32, (tq, window), 0)
    allowed = (key_idx >= st_ref[...]) & (key_idx <= row_idx)
    s = jnp.where(allowed, s, neg_large)
    row_top = jnp.max(s, axis=1, keepdims=True)
    log_total = row_top + jnp.log(jnp.sum(jnp.exp(s - row_top), axis=1, keepdims=True))
    p = jnp.exp(s - log_total)
    p_low = p.astype(jnp.bfloat16)
    ctx_ref[...] = jnp.dot(p_low, v, preferred_element_type=jnp.float32).astype(ctx_ref.dtype)
    dp = lax.dot_general(do, v, rows_t, preferred_element_type=jnp.float32)
    weighted = jnp.sum(p * dp, axis=1, keepdims=True)
    ds = (p * (dp - weighted)).astype(jnp.bfloat16)
    dq_ref[...] = (jnp.dot(ds, k, preferred_element_type=jnp.float32) * scale).astype(dq_ref.dtype)
    dk_scr[pl.ds(a, window), :] += lax.dot_general(ds, q, cols_t, preferred_element_type=jnp.float32)
    dv_scr[pl.ds(a, window), :] += lax.dot_general(p_low, do, cols_t, preferred_element_type=jnp.float32)

    @pl.when(qi == pl.num_programs(0) - 1)
    def _():
        hd = q_ref.shape[1]
        send_ref[:, :hd] = (dk_scr[:half, :] * scale).astype(send_ref.dtype)
        send_ref[:, hd:] = dv_scr[:half, :].astype(send_ref.dtype)
        keep_ref[:, :hd] = dk_scr[half:, :] * scale
        keep_ref[:, hd:] = dv_scr[half:, :]


def attention(queries, kv_prev, kv_own, grad_ctx, rel_start):
    rows, hd = queries.shape
    tq = 256
    window = rows + tq
    kernel = functools.partial(
        attention_kernel, tq=tq, window=window, shift=rows, scale=hd ** (-0.5)
    )
    q_spec = pl.BlockSpec((tq, hd), lambda i: (i, 0))
    k_spec = pl.BlockSpec((rows, hd), lambda i: (0, 0))
    v_spec = pl.BlockSpec((rows, hd), lambda i: (0, 1))
    kv_spec = pl.BlockSpec((rows, 2 * hd), lambda i: (0, 0))
    steps = rows // tq
    cost = pl.CostEstimate(
        flops=steps * 12 * tq * window * hd,
        transcendentals=steps * 2 * tq * window,
        bytes_accessed=rows * hd * 2 * 8 + rows * 2 * hd * 6,
    )
    return pl.pallas_call(
        kernel,
        grid=(steps,),
        in_specs=[q_spec, k_spec, v_spec, k_spec, v_spec, q_spec,
                  pl.BlockSpec((tq, 1), lambda i: (i, 0))],
        out_specs=[q_spec, q_spec, kv_spec, kv_spec],
        out_shape=[
            jax.ShapeDtypeStruct((rows, hd), jnp.bfloat16),
            jax.ShapeDtypeStruct((rows, hd), jnp.bfloat16),
            jax.ShapeDtypeStruct((rows, 2 * hd), jnp.bfloat16),
            jax.ShapeDtypeStruct((rows, 2 * hd), jnp.float32),
        ],
        scratch_shapes=[pltpu.VMEM((2 * rows, hd), jnp.bfloat16)] * 2
        + [pltpu.VMEM((2 * rows, hd), jnp.float32)] * 2,
        compiler_params=pltpu.CompilerParams(dimension_semantics=("arbitrary",)),
        cost_estimate=cost,
    )(queries, kv_prev, kv_prev, kv_own, kv_own, grad_ctx, rel_start)


def body(
    own_rows, gain, w_query, w_key, w_value, grad_context, send_slot, recv_slot, episode_start
):
    seq_count = lax.axis_size("seq")
    head_count = lax.axis_size("head")
    shard = lax.axis_index("seq")
    head_pos = lax.axis_index("head")
    row_count = own_rows.shape[0]
    capacity = 2 * row_count // seq_count
    width = own_rows.shape[1] // head_count
    own_part = lax.dynamic_slice_in_dim(own_rows, head_pos * width, width, 1)
    slots = seq_count * capacity
    send_pick = (
        lax.broadcasted_iota(jnp.int32, (slots, row_count), 0) == send_slot[None, :]
    ).astype(own_rows.dtype)
    outgoing = jnp.dot(send_pick, own_part, preferred_element_type=jnp.float32).astype(
        own_rows.dtype
    )
    arrived = lax.all_to_all(outgoing, "seq", split_axis=0, concat_axis=0, tiled=True)
    recv_pick = (
        lax.broadcasted_iota(jnp.int32, (row_count, slots), 1) == recv_slot[:, None]
    ).astype(own_rows.dtype)
    packed_part = jnp.dot(recv_pick, arrived, preferred_element_type=jnp.float32).astype(
        own_rows.dtype
    )
    packed = lax.all_gather(packed_part, "head", axis=1, tiled=True)
    rows_float = packed.astype(jnp.float32)
    inv_rms = lax.rsqrt(jnp.mean(rows_float * rows_float, axis=-1, keepdims=True) + epsilon)
    normed = (rows_float * inv_rms * gain).astype(jnp.bfloat16)
    queries = jnp.dot(normed, w_query, preferred_element_type=jnp.float32).astype(jnp.bfloat16)
    rel_start = (episode_start - (shard - 1) * row_count).reshape(row_count, 1)
    local_heads = queries.shape[1] // HD
    contexts, grad_queries, kv_parts = [], [], []
    for h in range(local_heads):
        cols = slice(h * HD, (h + 1) * HD)
        kv_weight = jnp.concatenate([w_key[:, cols], w_value[:, cols]], axis=1)
        kv_own = jnp.dot(normed, kv_weight, preferred_element_type=jnp.float32).astype(jnp.bfloat16)
        kv_sent = kv_own
        if h > 0:
            kv_sent, _ = lax.optimization_barrier((kv_own, kv_prev))
        kv_prev = passed_along(kv_sent, "seq", 1)
        context_h, grad_q_h, kv_send, kv_keep = attention(
            queries[:, cols], kv_prev, kv_own, grad_context[:, cols], rel_start
        )
        kv_next = passed_along(kv_send, "seq", -1)
        grad_kv = (kv_keep + kv_next.astype(jnp.float32)).astype(jnp.bfloat16)
        contexts.append(context_h)
        grad_queries.append(grad_q_h)
        kv_parts.append((grad_kv, kv_weight))
    context_out = jnp.concatenate(contexts, axis=1)
    grad_q_all = jnp.concatenate(grad_queries, axis=1)
    share = row_count // head_count

    def project(grads, weight):
        return jnp.einsum("rc,dc->rd", grads, weight, preferred_element_type=jnp.float32)

    term = project(grad_q_all, w_query)
    for grad_kv, kv_weight in kv_parts:
        term = term + project(grad_kv, kv_weight)
    grad_normed = lax.psum_scatter(
        term.astype(jnp.bfloat16),
        "head",
        scatter_dimension=0,
        tiled=True,
    ).astype(jnp.float32)
    own_start = head_pos * share
    mine = lax.dynamic_slice_in_dim(packed, own_start, share, 0).astype(jnp.float32)
    mine_inv = lax.dynamic_slice_in_dim(inv_rms, own_start, share, 0)
    gain_grad = gain * grad_normed
    mixed = jnp.mean(gain_grad * mine, axis=-1, keepdims=True)
    d_rows = (mine_inv * gain_grad - mine * mine_inv**3 * mixed).astype(jnp.bfloat16)
    return (context_out, d_rows)


def solution(mesh):
    in_specs = (
        P("seq", None),
        P(),
        P(None, "head"),
        P(None, "head"),
        P(None, "head"),
        P("seq", "head"),
        P("seq"),
        P("seq"),
        P("seq"),
    )
    out_specs = (P("seq", "head"), P(("seq", "head"), None))
    return jax.shard_map(body, mesh=mesh, in_specs=in_specs, out_specs=out_specs, check_vma=False)
```

```python
import functools

import jax
import jax.numpy as jnp
from jax import lax
from jax.experimental import pallas as pl
from jax.experimental.pallas import tpu as pltpu
from jax.sharding import PartitionSpec as P

HD = 128


neg_large = -1e30
epsilon = 1e-05


def passed_along(array, axis, by):
    count = lax.axis_size(axis)
    pairs = [(i, i + by) for i in range(count) if 0 <= i + by < count]
    return lax.ppermute(array, axis, pairs)


def block_terms(queries, keys_all, values_all, grad_ctx, starts, first_query, first_key):
    score_scale = queries.shape[-1] ** (-0.5)
    query_pos = first_query + jnp.arange(queries.shape[0], dtype=jnp.int32)
    key_pos = first_key + jnp.arange(keys_all.shape[0], dtype=jnp.int32)
    allowed = (key_pos[None, :] >= starts[:, None]) & (key_pos[None, :] <= query_pos[:, None])
    scores = (
        jnp.einsum("bhe,khe->bhk", queries, keys_all, preferred_element_type=jnp.float32)
        * score_scale
    )
    scores = jnp.where(allowed[:, None, :], scores, neg_large)
    row_top = jnp.max(scores, axis=-1, keepdims=True)
    log_total = row_top + jnp.log(jnp.sum(jnp.exp(scores - row_top), axis=-1, keepdims=True))
    probs = jnp.exp(scores - log_total)
    probs_low = probs.astype(jnp.bfloat16)
    context = jnp.einsum("bhk,khe->bhe", probs_low, values_all, preferred_element_type=jnp.float32)
    grad_probs = jnp.einsum(
        "bhe,khe->bhk", grad_ctx, values_all, preferred_element_type=jnp.float32
    )
    weighted = jnp.sum(probs * grad_probs, axis=-1, keepdims=True)
    grad_scores = (probs * (grad_probs - weighted)).astype(jnp.bfloat16)
    grad_q = (
        jnp.einsum("bhk,khe->bhe", grad_scores, keys_all, preferred_element_type=jnp.float32)
        * score_scale
    )
    grad_k = (
        jnp.einsum("bhk,bhe->khe", grad_scores, queries, preferred_element_type=jnp.float32)
        * score_scale
    )
    grad_v = jnp.einsum("bhk,bhe->khe", probs_low, grad_ctx, preferred_element_type=jnp.float32)
    return (context, grad_q, grad_k, grad_v)


def attention_kernel(
    q_ref, kp_ref, vp_ref, ko_ref, vo_ref, do_ref, st_ref,
    ctx_ref, dq_ref, send_ref, keep_ref,
    k_scr, v_scr, dk_scr, dv_scr, *, tq, window, shift, scale
):
    qi = pl.program_id(0)
    a = pl.multiple_of(qi * tq, tq)
    half = kp_ref.shape[0]

    @pl.when(qi == 0)
    def _():
        k_scr[:half, :] = kp_ref[...]
        k_scr[half:, :] = ko_ref[...]
        v_scr[:half, :] = vp_ref[...]
        v_scr[half:, :] = vo_ref[...]
        dk_scr[...] = jnp.zeros_like(dk_scr)
        dv_scr[...] = jnp.zeros_like(dv_scr)

    q = q_ref[...]
    k = k_scr[pl.ds(a, window), :]
    v = v_scr[pl.ds(a, window), :]
    do = do_ref[...]
    rows_t = (((1,), (1,)), ((), ()))
    cols_t = (((0,), (0,)), ((), ()))
    s = lax.dot_general(q, k, rows_t, preferred_element_type=jnp.float32) * scale
    key_idx = a + lax.broadcasted_iota(jnp.int32, (tq, window), 1)
    row_idx = a + shift + lax.broadcasted_iota(jnp.int32, (tq, window), 0)
    allowed = (key_idx >= st_ref[...]) & (key_idx <= row_idx)
    s = jnp.where(allowed, s, neg_large)
    row_top = jnp.max(s, axis=1, keepdims=True)
    e = jnp.exp(s - row_top)
    p = e * (1.0 / jnp.sum(e, axis=1, keepdims=True))
    p_low = p.astype(jnp.bfloat16)
    ctx_ref[...] = jnp.dot(p_low, v, preferred_element_type=jnp.float32).astype(ctx_ref.dtype)
    dp = lax.dot_general(do, v, rows_t, preferred_element_type=jnp.float32)
    weighted = jnp.sum(p * dp, axis=1, keepdims=True)
    ds = (p * (dp - weighted)).astype(jnp.bfloat16)
    dq_ref[...] = (jnp.dot(ds, k, preferred_element_type=jnp.float32) * scale).astype(dq_ref.dtype)
    dk_scr[pl.ds(a, window), :] += lax.dot_general(ds, q, cols_t, preferred_element_type=jnp.float32)
    dv_scr[pl.ds(a, window), :] += lax.dot_general(p_low, do, cols_t, preferred_element_type=jnp.float32)

    @pl.when(qi == pl.num_programs(0) - 1)
    def _():
        hd = q_ref.shape[1]
        send_ref[:, :hd] = (dk_scr[:half, :] * scale).astype(send_ref.dtype)
        send_ref[:, hd:] = dv_scr[:half, :].astype(send_ref.dtype)
        keep_ref[:, :hd] = dk_scr[half:, :] * scale
        keep_ref[:, hd:] = dv_scr[half:, :]


def attention(queries, kv_prev, kv_own, grad_ctx, rel_start):
    rows, hd = queries.shape
    tq = 256
    window = rows + tq
    kernel = functools.partial(
        attention_kernel, tq=tq, window=window, shift=rows, scale=hd ** (-0.5)
    )
    q_spec = pl.BlockSpec((tq, hd), lambda i: (i, 0))
    k_spec = pl.BlockSpec((rows, hd), lambda i: (0, 0))
    v_spec = pl.BlockSpec((rows, hd), lambda i: (0, 1))
    kv_spec = pl.BlockSpec((rows, 2 * hd), lambda i: (0, 0))
    steps = rows // tq
    cost = pl.CostEstimate(
        flops=steps * 12 * tq * window * hd,
        transcendentals=steps * 2 * tq * window,
        bytes_accessed=rows * hd * 2 * 8 + rows * 2 * hd * 6,
    )
    return pl.pallas_call(
        kernel,
        grid=(steps,),
        in_specs=[q_spec, k_spec, v_spec, k_spec, v_spec, q_spec,
                  pl.BlockSpec((tq, 1), lambda i: (i, 0))],
        out_specs=[q_spec, q_spec, kv_spec, kv_spec],
        out_shape=[
            jax.ShapeDtypeStruct((rows, hd), jnp.bfloat16),
            jax.ShapeDtypeStruct((rows, hd), jnp.bfloat16),
            jax.ShapeDtypeStruct((rows, 2 * hd), jnp.bfloat16),
            jax.ShapeDtypeStruct((rows, 2 * hd), jnp.float32),
        ],
        scratch_shapes=[pltpu.VMEM((2 * rows, hd), jnp.bfloat16)] * 2
        + [pltpu.VMEM((2 * rows, hd), jnp.float32)] * 2,
        compiler_params=pltpu.CompilerParams(dimension_semantics=("arbitrary",)),
        cost_estimate=cost,
    )(queries, kv_prev, kv_prev, kv_own, kv_own, grad_ctx, rel_start)


def body(
    own_rows, gain, w_query, w_key, w_value, grad_context, send_slot, recv_slot, episode_start
):
    seq_count = lax.axis_size("seq")
    head_count = lax.axis_size("head")
    shard = lax.axis_index("seq")
    head_pos = lax.axis_index("head")
    row_count = own_rows.shape[0]
    capacity = 2 * row_count // seq_count
    width = own_rows.shape[1] // head_count
    own_part = lax.dynamic_slice_in_dim(own_rows, head_pos * width, width, 1)
    slots = seq_count * capacity
    send_pick = (
        lax.broadcasted_iota(jnp.int32, (slots, row_count), 0) == send_slot[None, :]
    ).astype(own_rows.dtype)
    outgoing = jnp.dot(send_pick, own_part, preferred_element_type=jnp.float32).astype(
        own_rows.dtype
    )
    arrived = lax.all_to_all(outgoing, "seq", split_axis=0, concat_axis=0, tiled=True)
    recv_pick = (
        lax.broadcasted_iota(jnp.int32, (row_count, slots), 1) == recv_slot[:, None]
    ).astype(own_rows.dtype)
    packed_part = jnp.dot(recv_pick, arrived, preferred_element_type=jnp.float32).astype(
        own_rows.dtype
    )
    packed = lax.all_gather(packed_part, "head", axis=1, tiled=True)
    rows_float = packed.astype(jnp.float32)
    inv_rms = lax.rsqrt(jnp.mean(rows_float * rows_float, axis=-1, keepdims=True) + epsilon)
    normed = (rows_float * inv_rms * gain).astype(jnp.bfloat16)
    queries = jnp.dot(normed, w_query, preferred_element_type=jnp.float32).astype(jnp.bfloat16)
    rel_start = (episode_start - (shard - 1) * row_count).reshape(row_count, 1)
    local_heads = queries.shape[1] // HD
    contexts, grad_queries, kv_parts = [], [], []
    for h in range(local_heads):
        cols = slice(h * HD, (h + 1) * HD)
        kv_weight = jnp.concatenate([w_key[:, cols], w_value[:, cols]], axis=1)
        kv_own = jnp.dot(normed, kv_weight, preferred_element_type=jnp.float32).astype(jnp.bfloat16)
        kv_sent = kv_own
        if h > 0:
            kv_sent, _ = lax.optimization_barrier((kv_own, kv_prev))
        kv_prev = passed_along(kv_sent, "seq", 1)
        context_h, grad_q_h, kv_send, kv_keep = attention(
            queries[:, cols], kv_prev, kv_own, grad_context[:, cols], rel_start
        )
        kv_next = passed_along(kv_send, "seq", -1)
        grad_kv = (kv_keep + kv_next.astype(jnp.float32)).astype(jnp.bfloat16)
        contexts.append(context_h)
        grad_queries.append(grad_q_h)
        kv_parts.append((grad_kv, kv_weight))
    context_out = jnp.concatenate(contexts, axis=1)
    grad_q_all = jnp.concatenate(grad_queries, axis=1)
    share = row_count // head_count

    def project(grads, weight):
        return jnp.einsum("rc,dc->rd", grads, weight, preferred_element_type=jnp.float32)

    term = project(grad_q_all, w_query)
    for grad_kv, kv_weight in kv_parts:
        term = term + project(grad_kv, kv_weight)
    grad_normed = lax.psum_scatter(
        term.astype(jnp.bfloat16),
        "head",
        scatter_dimension=0,
        tiled=True,
    ).astype(jnp.float32)
    own_start = head_pos * share
    mine = lax.dynamic_slice_in_dim(packed, own_start, share, 0).astype(jnp.float32)
    mine_inv = lax.dynamic_slice_in_dim(inv_rms, own_start, share, 0)
    gain_grad = gain * grad_normed
    mixed = jnp.mean(gain_grad * mine, axis=-1, keepdims=True)
    d_rows = (mine_inv * gain_grad - mine * mine_inv**3 * mixed).astype(jnp.bfloat16)
    return (context_out, d_rows)


def solution(mesh):
    in_specs = (
        P("seq", None),
        P(),
        P(None, "head"),
        P(None, "head"),
        P(None, "head"),
        P("seq", "head"),
        P("seq"),
        P("seq"),
        P("seq"),
    )
    out_specs = (P("seq", "head"), P(("seq", "head"), None))
    return jax.shard_map(body, mesh=mesh, in_specs=in_specs, out_specs=out_specs, check_vma=False)
```

```python
import functools

import jax
import jax.numpy as jnp
from jax import lax
from jax.experimental import pallas as pl
from jax.experimental.pallas import tpu as pltpu
from jax.sharding import PartitionSpec as P

HD = 128


neg_large = -1e30
epsilon = 1e-05


def passed_along(array, axis, by):
    count = lax.axis_size(axis)
    pairs = [(i, i + by) for i in range(count) if 0 <= i + by < count]
    return lax.ppermute(array, axis, pairs)


def block_terms(queries, keys_all, values_all, grad_ctx, starts, first_query, first_key):
    score_scale = queries.shape[-1] ** (-0.5)
    query_pos = first_query + jnp.arange(queries.shape[0], dtype=jnp.int32)
    key_pos = first_key + jnp.arange(keys_all.shape[0], dtype=jnp.int32)
    allowed = (key_pos[None, :] >= starts[:, None]) & (key_pos[None, :] <= query_pos[:, None])
    scores = (
        jnp.einsum("bhe,khe->bhk", queries, keys_all, preferred_element_type=jnp.float32)
        * score_scale
    )
    scores = jnp.where(allowed[:, None, :], scores, neg_large)
    row_top = jnp.max(scores, axis=-1, keepdims=True)
    log_total = row_top + jnp.log(jnp.sum(jnp.exp(scores - row_top), axis=-1, keepdims=True))
    probs = jnp.exp(scores - log_total)
    probs_low = probs.astype(jnp.bfloat16)
    context = jnp.einsum("bhk,khe->bhe", probs_low, values_all, preferred_element_type=jnp.float32)
    grad_probs = jnp.einsum(
        "bhe,khe->bhk", grad_ctx, values_all, preferred_element_type=jnp.float32
    )
    weighted = jnp.sum(probs * grad_probs, axis=-1, keepdims=True)
    grad_scores = (probs * (grad_probs - weighted)).astype(jnp.bfloat16)
    grad_q = (
        jnp.einsum("bhk,khe->bhe", grad_scores, keys_all, preferred_element_type=jnp.float32)
        * score_scale
    )
    grad_k = (
        jnp.einsum("bhk,bhe->khe", grad_scores, queries, preferred_element_type=jnp.float32)
        * score_scale
    )
    grad_v = jnp.einsum("bhk,bhe->khe", probs_low, grad_ctx, preferred_element_type=jnp.float32)
    return (context, grad_q, grad_k, grad_v)


def attention_kernel(
    q_ref, kp_ref, vp_ref, ko_ref, vo_ref, do_ref, st_ref,
    ctx_ref, dq_ref, send_ref, keep_ref,
    k_scr, v_scr, dk_scr, dv_scr, *, tq, window, shift, scale
):
    qi = pl.program_id(0)
    a = pl.multiple_of(qi * tq, tq)
    half = kp_ref.shape[0]

    @pl.when(qi == 0)
    def _():
        k_scr[:half, :] = kp_ref[...]
        k_scr[half:, :] = ko_ref[...]
        v_scr[:half, :] = vp_ref[...]
        v_scr[half:, :] = vo_ref[...]
        dk_scr[...] = jnp.zeros_like(dk_scr)
        dv_scr[...] = jnp.zeros_like(dv_scr)

    q = q_ref[...]
    k = k_scr[pl.ds(a, window), :]
    v = v_scr[pl.ds(a, window), :]
    do = do_ref[...]
    rows_t = (((1,), (1,)), ((), ()))
    cols_t = (((0,), (0,)), ((), ()))
    s = lax.dot_general(q, k, rows_t, preferred_element_type=jnp.float32) * scale
    key_idx = a + lax.broadcasted_iota(jnp.int32, (tq, window), 1)
    row_idx = a + shift + lax.broadcasted_iota(jnp.int32, (tq, window), 0)
    allowed = (key_idx >= st_ref[...]) & (key_idx <= row_idx)
    s = jnp.where(allowed, s, neg_large)
    row_top = jnp.max(s, axis=1, keepdims=True)
    log_total = row_top + jnp.log(jnp.sum(jnp.exp(s - row_top), axis=1, keepdims=True))
    p = jnp.exp(s - log_total)
    p_low = p.astype(jnp.bfloat16)
    ctx_ref[...] = jnp.dot(p_low, v, preferred_element_type=jnp.float32).astype(ctx_ref.dtype)
    dp = lax.dot_general(do, v, rows_t, preferred_element_type=jnp.float32)
    weighted = jnp.sum(p * dp, axis=1, keepdims=True)
    ds = (p * (dp - weighted)).astype(jnp.bfloat16)
    dq_ref[...] = (jnp.dot(ds, k, preferred_element_type=jnp.float32) * scale).astype(dq_ref.dtype)
    dk_scr[pl.ds(a, window), :] += lax.dot_general(ds, q, cols_t, preferred_element_type=jnp.float32)
    dv_scr[pl.ds(a, window), :] += lax.dot_general(p_low, do, cols_t, preferred_element_type=jnp.float32)

    @pl.when(qi == pl.num_programs(0) - 1)
    def _():
        hd = q_ref.shape[1]
        send_ref[:, :hd] = (dk_scr[:half, :] * scale).astype(send_ref.dtype)
        send_ref[:, hd:] = dv_scr[:half, :].astype(send_ref.dtype)
        keep_ref[:, :hd] = dk_scr[half:, :] * scale
        keep_ref[:, hd:] = dv_scr[half:, :]


def attention(queries, kv_prev, kv_own, grad_ctx, rel_start):
    rows, hd = queries.shape
    tq = 128
    window = rows + tq
    kernel = functools.partial(
        attention_kernel, tq=tq, window=window, shift=rows, scale=hd ** (-0.5)
    )
    q_spec = pl.BlockSpec((tq, hd), lambda i: (i, 0))
    k_spec = pl.BlockSpec((rows, hd), lambda i: (0, 0))
    v_spec = pl.BlockSpec((rows, hd), lambda i: (0, 1))
    kv_spec = pl.BlockSpec((rows, 2 * hd), lambda i: (0, 0))
    steps = rows // tq
    cost = pl.CostEstimate(
        flops=steps * 12 * tq * window * hd,
        transcendentals=steps * 2 * tq * window,
        bytes_accessed=rows * hd * 2 * 8 + rows * 2 * hd * 6,
    )
    return pl.pallas_call(
        kernel,
        grid=(steps,),
        in_specs=[q_spec, k_spec, v_spec, k_spec, v_spec, q_spec,
                  pl.BlockSpec((tq, 1), lambda i: (i, 0))],
        out_specs=[q_spec, q_spec, kv_spec, kv_spec],
        out_shape=[
            jax.ShapeDtypeStruct((rows, hd), jnp.bfloat16),
            jax.ShapeDtypeStruct((rows, hd), jnp.bfloat16),
            jax.ShapeDtypeStruct((rows, 2 * hd), jnp.bfloat16),
            jax.ShapeDtypeStruct((rows, 2 * hd), jnp.float32),
        ],
        scratch_shapes=[pltpu.VMEM((2 * rows, hd), jnp.bfloat16)] * 2
        + [pltpu.VMEM((2 * rows, hd), jnp.float32)] * 2,
        compiler_params=pltpu.CompilerParams(dimension_semantics=("arbitrary",)),
        cost_estimate=cost,
    )(queries, kv_prev, kv_prev, kv_own, kv_own, grad_ctx, rel_start)


def body(
    own_rows, gain, w_query, w_key, w_value, grad_context, send_slot, recv_slot, episode_start
):
    seq_count = lax.axis_size("seq")
    head_count = lax.axis_size("head")
    shard = lax.axis_index("seq")
    head_pos = lax.axis_index("head")
    row_count = own_rows.shape[0]
    capacity = 2 * row_count // seq_count
    width = own_rows.shape[1] // head_count
    own_part = lax.dynamic_slice_in_dim(own_rows, head_pos * width, width, 1)
    slots = seq_count * capacity
    send_pick = (
        lax.broadcasted_iota(jnp.int32, (slots, row_count), 0) == send_slot[None, :]
    ).astype(own_rows.dtype)
    outgoing = jnp.dot(send_pick, own_part, preferred_element_type=jnp.float32).astype(
        own_rows.dtype
    )
    arrived = lax.all_to_all(outgoing, "seq", split_axis=0, concat_axis=0, tiled=True)
    recv_pick = (
        lax.broadcasted_iota(jnp.int32, (row_count, slots), 1) == recv_slot[:, None]
    ).astype(own_rows.dtype)
    packed_part = jnp.dot(recv_pick, arrived, preferred_element_type=jnp.float32).astype(
        own_rows.dtype
    )
    packed = lax.all_gather(packed_part, "head", axis=1, tiled=True)
    rows_float = packed.astype(jnp.float32)
    inv_rms = lax.rsqrt(jnp.mean(rows_float * rows_float, axis=-1, keepdims=True) + epsilon)
    normed = (rows_float * inv_rms * gain).astype(jnp.bfloat16)
    queries = jnp.dot(normed, w_query, preferred_element_type=jnp.float32).astype(jnp.bfloat16)
    rel_start = (episode_start - (shard - 1) * row_count).reshape(row_count, 1)
    local_heads = queries.shape[1] // HD
    contexts, grad_queries, kv_parts = [], [], []
    for h in range(local_heads):
        cols = slice(h * HD, (h + 1) * HD)
        kv_weight = jnp.concatenate([w_key[:, cols], w_value[:, cols]], axis=1)
        kv_own = jnp.dot(normed, kv_weight, preferred_element_type=jnp.float32).astype(jnp.bfloat16)
        kv_sent = kv_own
        if h > 0:
            kv_sent, _ = lax.optimization_barrier((kv_own, kv_prev))
        kv_prev = passed_along(kv_sent, "seq", 1)
        context_h, grad_q_h, kv_send, kv_keep = attention(
            queries[:, cols], kv_prev, kv_own, grad_context[:, cols], rel_start
        )
        kv_next = passed_along(kv_send, "seq", -1)
        grad_kv = (kv_keep + kv_next.astype(jnp.float32)).astype(jnp.bfloat16)
        contexts.append(context_h)
        grad_queries.append(grad_q_h)
        kv_parts.append((grad_kv, kv_weight))
    context_out = jnp.concatenate(contexts, axis=1)
    grad_q_all = jnp.concatenate(grad_queries, axis=1)
    share = row_count // head_count

    def project(grads, weight):
        return jnp.einsum("rc,dc->rd", grads, weight, preferred_element_type=jnp.float32)

    term = project(grad_q_all, w_query)
    for grad_kv, kv_weight in kv_parts:
        term = term + project(grad_kv, kv_weight)
    grad_normed = lax.psum_scatter(
        term.astype(jnp.bfloat16),
        "head",
        scatter_dimension=0,
        tiled=True,
    ).astype(jnp.float32)
    own_start = head_pos * share
    mine = lax.dynamic_slice_in_dim(packed, own_start, share, 0).astype(jnp.float32)
    mine_inv = lax.dynamic_slice_in_dim(inv_rms, own_start, share, 0)
    gain_grad = gain * grad_normed
    mixed = jnp.mean(gain_grad * mine, axis=-1, keepdims=True)
    d_rows = (mine_inv * gain_grad - mine * mine_inv**3 * mixed).astype(jnp.bfloat16)
    return (context_out, d_rows)


def solution(mesh):
    in_specs = (
        P("seq", None),
        P(),
        P(None, "head"),
        P(None, "head"),
        P(None, "head"),
        P("seq", "head"),
        P("seq"),
        P("seq"),
        P("seq"),
    )
    out_specs = (P("seq", "head"), P(("seq", "head"), None))
    return jax.shard_map(body, mesh=mesh, in_specs=in_specs, out_specs=out_specs, check_vma=False)
```

```python
import functools

import jax
import jax.numpy as jnp
from jax import lax
from jax.experimental import pallas as pl
from jax.experimental.pallas import tpu as pltpu
from jax.sharding import PartitionSpec as P

HD = 128


neg_large = -1e30
epsilon = 1e-05


def passed_along(array, axis, by):
    count = lax.axis_size(axis)
    pairs = [(i, i + by) for i in range(count) if 0 <= i + by < count]
    return lax.ppermute(array, axis, pairs)


def block_terms(queries, keys_all, values_all, grad_ctx, starts, first_query, first_key):
    score_scale = queries.shape[-1] ** (-0.5)
    query_pos = first_query + jnp.arange(queries.shape[0], dtype=jnp.int32)
    key_pos = first_key + jnp.arange(keys_all.shape[0], dtype=jnp.int32)
    allowed = (key_pos[None, :] >= starts[:, None]) & (key_pos[None, :] <= query_pos[:, None])
    scores = (
        jnp.einsum("bhe,khe->bhk", queries, keys_all, preferred_element_type=jnp.float32)
        * score_scale
    )
    scores = jnp.where(allowed[:, None, :], scores, neg_large)
    row_top = jnp.max(scores, axis=-1, keepdims=True)
    log_total = row_top + jnp.log(jnp.sum(jnp.exp(scores - row_top), axis=-1, keepdims=True))
    probs = jnp.exp(scores - log_total)
    probs_low = probs.astype(jnp.bfloat16)
    context = jnp.einsum("bhk,khe->bhe", probs_low, values_all, preferred_element_type=jnp.float32)
    grad_probs = jnp.einsum(
        "bhe,khe->bhk", grad_ctx, values_all, preferred_element_type=jnp.float32
    )
    weighted = jnp.sum(probs * grad_probs, axis=-1, keepdims=True)
    grad_scores = (probs * (grad_probs - weighted)).astype(jnp.bfloat16)
    grad_q = (
        jnp.einsum("bhk,khe->bhe", grad_scores, keys_all, preferred_element_type=jnp.float32)
        * score_scale
    )
    grad_k = (
        jnp.einsum("bhk,bhe->khe", grad_scores, queries, preferred_element_type=jnp.float32)
        * score_scale
    )
    grad_v = jnp.einsum("bhk,bhe->khe", probs_low, grad_ctx, preferred_element_type=jnp.float32)
    return (context, grad_q, grad_k, grad_v)


def attention_kernel(
    q_ref, kp_ref, vp_ref, ko_ref, vo_ref, do_ref, st_ref,
    ctx_ref, dq_ref, send_ref, keep_ref,
    k_scr, v_scr, dk_scr, dv_scr, *, tq, window, shift, scale
):
    qi = pl.program_id(0)
    a = pl.multiple_of(qi * tq, tq)
    half = kp_ref.shape[0]

    @pl.when(qi == 0)
    def _():
        k_scr[:half, :] = kp_ref[...]
        k_scr[half:, :] = ko_ref[...]
        v_scr[:half, :] = vp_ref[...]
        v_scr[half:, :] = vo_ref[...]
        dk_scr[...] = jnp.zeros_like(dk_scr)
        dv_scr[...] = jnp.zeros_like(dv_scr)

    q = q_ref[...]
    k = k_scr[pl.ds(a, window), :]
    v = v_scr[pl.ds(a, window), :]
    do = do_ref[...]
    rows_t = (((1,), (1,)), ((), ()))
    cols_t = (((0,), (0,)), ((), ()))
    s = lax.dot_general(q, k, rows_t, preferred_element_type=jnp.float32) * scale
    key_off = lax.broadcasted_iota(jnp.int32, (tq, window), 1)
    row_off = lax.broadcasted_iota(jnp.int32, (tq, window), 0)
    allowed = (key_off >= st_ref[...] - a) & (key_off - row_off <= shift)
    s = jnp.where(allowed, s, neg_large)
    row_top = jnp.max(s, axis=1, keepdims=True)
    log_total = row_top + jnp.log(jnp.sum(jnp.exp(s - row_top), axis=1, keepdims=True))
    p = jnp.exp(s - log_total)
    p_low = p.astype(jnp.bfloat16)
    ctx_ref[...] = jnp.dot(p_low, v, preferred_element_type=jnp.float32).astype(ctx_ref.dtype)
    dp = lax.dot_general(do, v, rows_t, preferred_element_type=jnp.float32)
    weighted = jnp.sum(p * dp, axis=1, keepdims=True)
    ds = (p * (dp - weighted)).astype(jnp.bfloat16)
    dq_ref[...] = (jnp.dot(ds, k, preferred_element_type=jnp.float32) * scale).astype(dq_ref.dtype)
    dk_scr[pl.ds(a, window), :] += lax.dot_general(ds, q, cols_t, preferred_element_type=jnp.float32)
    dv_scr[pl.ds(a, window), :] += lax.dot_general(p_low, do, cols_t, preferred_element_type=jnp.float32)

    @pl.when(qi == pl.num_programs(0) - 1)
    def _():
        hd = q_ref.shape[1]
        send_ref[:, :hd] = (dk_scr[:half, :] * scale).astype(send_ref.dtype)
        send_ref[:, hd:] = dv_scr[:half, :].astype(send_ref.dtype)
        keep_ref[:, :hd] = dk_scr[half:, :] * scale
        keep_ref[:, hd:] = dv_scr[half:, :]


def attention(queries, kv_prev, kv_own, grad_ctx, rel_start):
    rows, hd = queries.shape
    tq = 256
    window = rows + tq
    kernel = functools.partial(
        attention_kernel, tq=tq, window=window, shift=rows, scale=hd ** (-0.5)
    )
    q_spec = pl.BlockSpec((tq, hd), lambda i: (i, 0))
    k_spec = pl.BlockSpec((rows, hd), lambda i: (0, 0))
    v_spec = pl.BlockSpec((rows, hd), lambda i: (0, 1))
    kv_spec = pl.BlockSpec((rows, 2 * hd), lambda i: (0, 0))
    steps = rows // tq
    cost = pl.CostEstimate(
        flops=steps * 12 * tq * window * hd,
        transcendentals=steps * 2 * tq * window,
        bytes_accessed=rows * hd * 2 * 8 + rows * 2 * hd * 6,
    )
    return pl.pallas_call(
        kernel,
        grid=(steps,),
        in_specs=[q_spec, k_spec, v_spec, k_spec, v_spec, q_spec,
                  pl.BlockSpec((tq, 1), lambda i: (i, 0))],
        out_specs=[q_spec, q_spec, kv_spec, kv_spec],
        out_shape=[
            jax.ShapeDtypeStruct((rows, hd), jnp.bfloat16),
            jax.ShapeDtypeStruct((rows, hd), jnp.bfloat16),
            jax.ShapeDtypeStruct((rows, 2 * hd), jnp.bfloat16),
            jax.ShapeDtypeStruct((rows, 2 * hd), jnp.float32),
        ],
        scratch_shapes=[pltpu.VMEM((2 * rows, hd), jnp.bfloat16)] * 2
        + [pltpu.VMEM((2 * rows, hd), jnp.float32)] * 2,
        compiler_params=pltpu.CompilerParams(dimension_semantics=("arbitrary",)),
        cost_estimate=cost,
    )(queries, kv_prev, kv_prev, kv_own, kv_own, grad_ctx, rel_start)


def body(
    own_rows, gain, w_query, w_key, w_value, grad_context, send_slot, recv_slot, episode_start
):
    seq_count = lax.axis_size("seq")
    head_count = lax.axis_size("head")
    shard = lax.axis_index("seq")
    head_pos = lax.axis_index("head")
    row_count = own_rows.shape[0]
    capacity = 2 * row_count // seq_count
    width = own_rows.shape[1] // head_count
    own_part = lax.dynamic_slice_in_dim(own_rows, head_pos * width, width, 1)
    slots = seq_count * capacity
    send_pick = (
        lax.broadcasted_iota(jnp.int32, (slots, row_count), 0) == send_slot[None, :]
    ).astype(own_rows.dtype)
    outgoing = jnp.dot(send_pick, own_part, preferred_element_type=jnp.float32).astype(
        own_rows.dtype
    )
    arrived = lax.all_to_all(outgoing, "seq", split_axis=0, concat_axis=0, tiled=True)
    recv_pick = (
        lax.broadcasted_iota(jnp.int32, (row_count, slots), 1) == recv_slot[:, None]
    ).astype(own_rows.dtype)
    packed_part = jnp.dot(recv_pick, arrived, preferred_element_type=jnp.float32).astype(
        own_rows.dtype
    )
    packed = lax.all_gather(packed_part, "head", axis=1, tiled=True)
    rows_float = packed.astype(jnp.float32)
    inv_rms = lax.rsqrt(jnp.mean(rows_float * rows_float, axis=-1, keepdims=True) + epsilon)
    normed = (rows_float * inv_rms * gain).astype(jnp.bfloat16)
    queries = jnp.dot(normed, w_query, preferred_element_type=jnp.float32).astype(jnp.bfloat16)
    rel_start = (episode_start - (shard - 1) * row_count).reshape(row_count, 1)
    local_heads = queries.shape[1] // HD
    contexts, grad_queries, kv_parts = [], [], []
    for h in range(local_heads):
        cols = slice(h * HD, (h + 1) * HD)
        kv_weight = jnp.concatenate([w_key[:, cols], w_value[:, cols]], axis=1)
        kv_own = jnp.dot(normed, kv_weight, preferred_element_type=jnp.float32).astype(jnp.bfloat16)
        kv_sent = kv_own
        if h > 0:
            kv_sent, _ = lax.optimization_barrier((kv_own, kv_prev))
        kv_prev = passed_along(kv_sent, "seq", 1)
        context_h, grad_q_h, kv_send, kv_keep = attention(
            queries[:, cols], kv_prev, kv_own, grad_context[:, cols], rel_start
        )
        kv_next = passed_along(kv_send, "seq", -1)
        grad_kv = (kv_keep + kv_next.astype(jnp.float32)).astype(jnp.bfloat16)
        contexts.append(context_h)
        grad_queries.append(grad_q_h)
        kv_parts.append((grad_kv, kv_weight))
    context_out = jnp.concatenate(contexts, axis=1)
    grad_q_all = jnp.concatenate(grad_queries, axis=1)
    share = row_count // head_count

    def project(grads, weight):
        return jnp.einsum("rc,dc->rd", grads, weight, preferred_element_type=jnp.float32)

    term = project(grad_q_all, w_query)
    for grad_kv, kv_weight in kv_parts:
        term = term + project(grad_kv, kv_weight)
    grad_normed = lax.psum_scatter(
        term.astype(jnp.bfloat16),
        "head",
        scatter_dimension=0,
        tiled=True,
    ).astype(jnp.float32)
    own_start = head_pos * share
    mine = lax.dynamic_slice_in_dim(packed, own_start, share, 0).astype(jnp.float32)
    mine_inv = lax.dynamic_slice_in_dim(inv_rms, own_start, share, 0)
    gain_grad = gain * grad_normed
    mixed = jnp.mean(gain_grad * mine, axis=-1, keepdims=True)
    d_rows = (mine_inv * gain_grad - mine * mine_inv**3 * mixed).astype(jnp.bfloat16)
    return (context_out, d_rows)


def solution(mesh):
    in_specs = (
        P("seq", None),
        P(),
        P(None, "head"),
        P(None, "head"),
        P(None, "head"),
        P("seq", "head"),
        P("seq"),
        P("seq"),
        P("seq"),
    )
    out_specs = (P("seq", "head"), P(("seq", "head"), None))
    return jax.shard_map(body, mesh=mesh, in_specs=in_specs, out_specs=out_specs, check_vma=False)
```

```python
import functools

import jax
import jax.numpy as jnp
from jax import lax
from jax.experimental import pallas as pl
from jax.experimental.pallas import tpu as pltpu
from jax.sharding import PartitionSpec as P

HD = 128


neg_large = -1e30
epsilon = 1e-05


def passed_along(array, axis, by):
    count = lax.axis_size(axis)
    pairs = [(i, i + by) for i in range(count) if 0 <= i + by < count]
    return lax.ppermute(array, axis, pairs)


def block_terms(queries, keys_all, values_all, grad_ctx, starts, first_query, first_key):
    score_scale = queries.shape[-1] ** (-0.5)
    query_pos = first_query + jnp.arange(queries.shape[0], dtype=jnp.int32)
    key_pos = first_key + jnp.arange(keys_all.shape[0], dtype=jnp.int32)
    allowed = (key_pos[None, :] >= starts[:, None]) & (key_pos[None, :] <= query_pos[:, None])
    scores = (
        jnp.einsum("bhe,khe->bhk", queries, keys_all, preferred_element_type=jnp.float32)
        * score_scale
    )
    scores = jnp.where(allowed[:, None, :], scores, neg_large)
    row_top = jnp.max(scores, axis=-1, keepdims=True)
    log_total = row_top + jnp.log(jnp.sum(jnp.exp(scores - row_top), axis=-1, keepdims=True))
    probs = jnp.exp(scores - log_total)
    probs_low = probs.astype(jnp.bfloat16)
    context = jnp.einsum("bhk,khe->bhe", probs_low, values_all, preferred_element_type=jnp.float32)
    grad_probs = jnp.einsum(
        "bhe,khe->bhk", grad_ctx, values_all, preferred_element_type=jnp.float32
    )
    weighted = jnp.sum(probs * grad_probs, axis=-1, keepdims=True)
    grad_scores = (probs * (grad_probs - weighted)).astype(jnp.bfloat16)
    grad_q = (
        jnp.einsum("bhk,khe->bhe", grad_scores, keys_all, preferred_element_type=jnp.float32)
        * score_scale
    )
    grad_k = (
        jnp.einsum("bhk,bhe->khe", grad_scores, queries, preferred_element_type=jnp.float32)
        * score_scale
    )
    grad_v = jnp.einsum("bhk,bhe->khe", probs_low, grad_ctx, preferred_element_type=jnp.float32)
    return (context, grad_q, grad_k, grad_v)


def attention_kernel(
    q_ref, kp_ref, vp_ref, ko_ref, vo_ref, do_ref, st_ref,
    ctx_ref, dq_ref, send_ref, keep_ref,
    k_scr, kt_scr, vt_scr, dk_scr, dv_scr, *, tq, window, shift, scale
):
    qi = pl.program_id(0)
    a = pl.multiple_of(qi * tq, tq)
    half = kp_ref.shape[0]

    @pl.when(qi == 0)
    def _():
        k_scr[:half, :] = kp_ref[...]
        k_scr[half:, :] = ko_ref[...]
        kt_scr[:, :half] = kp_ref[...].T
        kt_scr[:, half:] = ko_ref[...].T
        vt_scr[:, :half] = vp_ref[...].T
        vt_scr[:, half:] = vo_ref[...].T
        dk_scr[...] = jnp.zeros_like(dk_scr)
        dv_scr[...] = jnp.zeros_like(dv_scr)

    q = q_ref[...]
    k = k_scr[pl.ds(a, window), :]
    kt = kt_scr[:, pl.ds(a, window)]
    vt = vt_scr[:, pl.ds(a, window)]
    do = do_ref[...]
    s = jnp.dot(q, kt, preferred_element_type=jnp.float32) * scale
    key_off = lax.broadcasted_iota(jnp.int32, (tq, window), 1)
    row_off = lax.broadcasted_iota(jnp.int32, (tq, window), 0)
    allowed = (key_off >= st_ref[...] - a) & (key_off - row_off <= shift)
    s = jnp.where(allowed, s, neg_large)
    row_top = jnp.max(s, axis=1, keepdims=True)
    log_total = row_top + jnp.log(jnp.sum(jnp.exp(s - row_top), axis=1, keepdims=True))
    p = jnp.exp(s - log_total)
    p_low = p.astype(jnp.bfloat16)
    ctx_ref[...] = lax.dot_general(
        p_low, vt, (((1,), (1,)), ((), ())), preferred_element_type=jnp.float32
    ).astype(ctx_ref.dtype)
    dp = jnp.dot(do, vt, preferred_element_type=jnp.float32)
    weighted = jnp.sum(p * dp, axis=1, keepdims=True)
    ds = (p * (dp - weighted)).astype(jnp.bfloat16)
    dq_ref[...] = (jnp.dot(ds, k, preferred_element_type=jnp.float32) * scale).astype(dq_ref.dtype)
    dk_scr[:, pl.ds(a, window)] += jnp.dot(q.T, ds, preferred_element_type=jnp.float32)
    dv_scr[:, pl.ds(a, window)] += jnp.dot(do.T, p_low, preferred_element_type=jnp.float32)

    @pl.when(qi == pl.num_programs(0) - 1)
    def _():
        hd = q_ref.shape[1]
        send_ref[:, :hd] = (dk_scr[:, :half].T * scale).astype(send_ref.dtype)
        send_ref[:, hd:] = dv_scr[:, :half].T.astype(send_ref.dtype)
        keep_ref[:, :hd] = dk_scr[:, half:].T * scale
        keep_ref[:, hd:] = dv_scr[:, half:].T


def attention(queries, kv_prev, kv_own, grad_ctx, rel_start):
    rows, hd = queries.shape
    tq = 256
    window = rows + tq
    kernel = functools.partial(
        attention_kernel, tq=tq, window=window, shift=rows, scale=hd ** (-0.5)
    )
    q_spec = pl.BlockSpec((tq, hd), lambda i: (i, 0))
    k_spec = pl.BlockSpec((rows, hd), lambda i: (0, 0))
    v_spec = pl.BlockSpec((rows, hd), lambda i: (0, 1))
    kv_spec = pl.BlockSpec((rows, 2 * hd), lambda i: (0, 0))
    steps = rows // tq
    cost = pl.CostEstimate(
        flops=steps * 12 * tq * window * hd,
        transcendentals=steps * 2 * tq * window,
        bytes_accessed=rows * hd * 2 * 8 + rows * 2 * hd * 6,
    )
    return pl.pallas_call(
        kernel,
        grid=(steps,),
        in_specs=[q_spec, k_spec, v_spec, k_spec, v_spec, q_spec,
                  pl.BlockSpec((tq, 1), lambda i: (i, 0))],
        out_specs=[q_spec, q_spec, kv_spec, kv_spec],
        out_shape=[
            jax.ShapeDtypeStruct((rows, hd), jnp.bfloat16),
            jax.ShapeDtypeStruct((rows, hd), jnp.bfloat16),
            jax.ShapeDtypeStruct((rows, 2 * hd), jnp.bfloat16),
            jax.ShapeDtypeStruct((rows, 2 * hd), jnp.float32),
        ],
        scratch_shapes=[pltpu.VMEM((2 * rows, hd), jnp.bfloat16)]
        + [pltpu.VMEM((hd, 2 * rows), jnp.bfloat16)] * 2
        + [pltpu.VMEM((hd, 2 * rows), jnp.float32)] * 2,
        compiler_params=pltpu.CompilerParams(dimension_semantics=("arbitrary",)),
        cost_estimate=cost,
    )(queries, kv_prev, kv_prev, kv_own, kv_own, grad_ctx, rel_start)


def body(
    own_rows, gain, w_query, w_key, w_value, grad_context, send_slot, recv_slot, episode_start
):
    seq_count = lax.axis_size("seq")
    head_count = lax.axis_size("head")
    shard = lax.axis_index("seq")
    head_pos = lax.axis_index("head")
    row_count = own_rows.shape[0]
    capacity = 2 * row_count // seq_count
    width = own_rows.shape[1] // head_count
    own_part = lax.dynamic_slice_in_dim(own_rows, head_pos * width, width, 1)
    slots = seq_count * capacity
    send_pick = (
        lax.broadcasted_iota(jnp.int32, (slots, row_count), 0) == send_slot[None, :]
    ).astype(own_rows.dtype)
    outgoing = jnp.dot(send_pick, own_part, preferred_element_type=jnp.float32).astype(
        own_rows.dtype
    )
    arrived = lax.all_to_all(outgoing, "seq", split_axis=0, concat_axis=0, tiled=True)
    recv_pick = (
        lax.broadcasted_iota(jnp.int32, (row_count, slots), 1) == recv_slot[:, None]
    ).astype(own_rows.dtype)
    packed_part = jnp.dot(recv_pick, arrived, preferred_element_type=jnp.float32).astype(
        own_rows.dtype
    )
    packed = lax.all_gather(packed_part, "head", axis=1, tiled=True)
    rows_float = packed.astype(jnp.float32)
    inv_rms = lax.rsqrt(jnp.mean(rows_float * rows_float, axis=-1, keepdims=True) + epsilon)
    normed = (rows_float * inv_rms * gain).astype(jnp.bfloat16)
    queries = jnp.dot(normed, w_query, preferred_element_type=jnp.float32).astype(jnp.bfloat16)
    rel_start = (episode_start - (shard - 1) * row_count).reshape(row_count, 1)
    local_heads = queries.shape[1] // HD
    contexts, grad_queries, kv_parts = [], [], []
    for h in range(local_heads):
        cols = slice(h * HD, (h + 1) * HD)
        kv_weight = jnp.concatenate([w_key[:, cols], w_value[:, cols]], axis=1)
        kv_own = jnp.dot(normed, kv_weight, preferred_element_type=jnp.float32).astype(jnp.bfloat16)
        kv_sent = kv_own
        if h > 0:
            kv_sent, _ = lax.optimization_barrier((kv_own, kv_prev))
        kv_prev = passed_along(kv_sent, "seq", 1)
        context_h, grad_q_h, kv_send, kv_keep = attention(
            queries[:, cols], kv_prev, kv_own, grad_context[:, cols], rel_start
        )
        kv_next = passed_along(kv_send, "seq", -1)
        grad_kv = (kv_keep + kv_next.astype(jnp.float32)).astype(jnp.bfloat16)
        contexts.append(context_h)
        grad_queries.append(grad_q_h)
        kv_parts.append((grad_kv, kv_weight))
    context_out = jnp.concatenate(contexts, axis=1)
    grad_q_all = jnp.concatenate(grad_queries, axis=1)
    share = row_count // head_count

    def project(grads, weight):
        return jnp.einsum("rc,dc->rd", grads, weight, preferred_element_type=jnp.float32)

    term = project(grad_q_all, w_query)
    for grad_kv, kv_weight in kv_parts:
        term = term + project(grad_kv, kv_weight)
    grad_normed = lax.psum_scatter(
        term.astype(jnp.bfloat16),
        "head",
        scatter_dimension=0,
        tiled=True,
    ).astype(jnp.float32)
    own_start = head_pos * share
    mine = lax.dynamic_slice_in_dim(packed, own_start, share, 0).astype(jnp.float32)
    mine_inv = lax.dynamic_slice_in_dim(inv_rms, own_start, share, 0)
    gain_grad = gain * grad_normed
    mixed = jnp.mean(gain_grad * mine, axis=-1, keepdims=True)
    d_rows = (mine_inv * gain_grad - mine * mine_inv**3 * mixed).astype(jnp.bfloat16)
    return (context_out, d_rows)


def solution(mesh):
    in_specs = (
        P("seq", None),
        P(),
        P(None, "head"),
        P(None, "head"),
        P(None, "head"),
        P("seq", "head"),
        P("seq"),
        P("seq"),
        P("seq"),
    )
    out_specs = (P("seq", "head"), P(("seq", "head"), None))
    return jax.shard_map(body, mesh=mesh, in_specs=in_specs, out_specs=out_specs, check_vma=False)
```

```python
import functools

import jax
import jax.numpy as jnp
from jax import lax
from jax.experimental import pallas as pl
from jax.experimental.pallas import tpu as pltpu
from jax.sharding import PartitionSpec as P

HD = 128


neg_large = -1e30
epsilon = 1e-05


def passed_along(array, axis, by):
    count = lax.axis_size(axis)
    pairs = [(i, i + by) for i in range(count) if 0 <= i + by < count]
    return lax.ppermute(array, axis, pairs)


def block_terms(queries, keys_all, values_all, grad_ctx, starts, first_query, first_key):
    score_scale = queries.shape[-1] ** (-0.5)
    query_pos = first_query + jnp.arange(queries.shape[0], dtype=jnp.int32)
    key_pos = first_key + jnp.arange(keys_all.shape[0], dtype=jnp.int32)
    allowed = (key_pos[None, :] >= starts[:, None]) & (key_pos[None, :] <= query_pos[:, None])
    scores = (
        jnp.einsum("bhe,khe->bhk", queries, keys_all, preferred_element_type=jnp.float32)
        * score_scale
    )
    scores = jnp.where(allowed[:, None, :], scores, neg_large)
    row_top = jnp.max(scores, axis=-1, keepdims=True)
    log_total = row_top + jnp.log(jnp.sum(jnp.exp(scores - row_top), axis=-1, keepdims=True))
    probs = jnp.exp(scores - log_total)
    probs_low = probs.astype(jnp.bfloat16)
    context = jnp.einsum("bhk,khe->bhe", probs_low, values_all, preferred_element_type=jnp.float32)
    grad_probs = jnp.einsum(
        "bhe,khe->bhk", grad_ctx, values_all, preferred_element_type=jnp.float32
    )
    weighted = jnp.sum(probs * grad_probs, axis=-1, keepdims=True)
    grad_scores = (probs * (grad_probs - weighted)).astype(jnp.bfloat16)
    grad_q = (
        jnp.einsum("bhk,khe->bhe", grad_scores, keys_all, preferred_element_type=jnp.float32)
        * score_scale
    )
    grad_k = (
        jnp.einsum("bhk,bhe->khe", grad_scores, queries, preferred_element_type=jnp.float32)
        * score_scale
    )
    grad_v = jnp.einsum("bhk,bhe->khe", probs_low, grad_ctx, preferred_element_type=jnp.float32)
    return (context, grad_q, grad_k, grad_v)


def attention_kernel(
    q_ref, kp_ref, vp_ref, ko_ref, vo_ref, do_ref, st_ref,
    ctx_ref, dq_ref, send_ref, keep_ref,
    k_scr, kt_scr, vt_scr, dk_scr, dv_scr, *, tq, window, shift, scale
):
    qi = pl.program_id(0)
    a = pl.multiple_of(qi * tq, tq)
    half = kp_ref.shape[0]

    @pl.when(qi == 0)
    def _():
        k_scr[:half, :] = kp_ref[...]
        k_scr[half:, :] = ko_ref[...]
        kt_scr[:, :half] = kp_ref[...].T
        kt_scr[:, half:] = ko_ref[...].T
        vt_scr[:, :half] = vp_ref[...].T
        vt_scr[:, half:] = vo_ref[...].T
        dk_scr[...] = jnp.zeros_like(dk_scr)
        dv_scr[...] = jnp.zeros_like(dv_scr)

    q = q_ref[...]
    k = k_scr[pl.ds(a, window), :]
    kt = kt_scr[:, pl.ds(a, window)]
    vt = vt_scr[:, pl.ds(a, window)]
    do = do_ref[...]
    s = jnp.dot(q, kt, preferred_element_type=jnp.float32) * scale
    key_off = lax.broadcasted_iota(jnp.int32, (tq, window), 1)
    row_off = lax.broadcasted_iota(jnp.int32, (tq, window), 0)
    allowed = (key_off >= st_ref[...] - a) & (key_off - row_off <= shift)
    s = jnp.where(allowed, s, neg_large)
    row_top = jnp.max(s, axis=1, keepdims=True)
    log_total = row_top + jnp.log(jnp.sum(jnp.exp(s - row_top), axis=1, keepdims=True))
    p = jnp.exp(s - log_total)
    p_low = p.astype(jnp.bfloat16)
    ctx_ref[...] = lax.dot_general(
        p_low, vt, (((1,), (1,)), ((), ())), preferred_element_type=jnp.float32
    ).astype(ctx_ref.dtype)
    dp = jnp.dot(do, vt, preferred_element_type=jnp.float32)
    weighted = jnp.sum(p * dp, axis=1, keepdims=True)
    ds = (p * (dp - weighted)).astype(jnp.bfloat16)
    dq_ref[...] = (jnp.dot(ds, k, preferred_element_type=jnp.float32) * scale).astype(dq_ref.dtype)
    dk_scr[:, pl.ds(a, window)] += jnp.dot(q.T, ds, preferred_element_type=jnp.float32)
    dv_scr[:, pl.ds(a, window)] += jnp.dot(do.T, p_low, preferred_element_type=jnp.float32)

    @pl.when(qi == pl.num_programs(0) - 1)
    def _():
        hd = q_ref.shape[1]
        send_ref[:, :hd] = (dk_scr[:, :half].T * scale).astype(send_ref.dtype)
        send_ref[:, hd:] = dv_scr[:, :half].T.astype(send_ref.dtype)
        keep_ref[:, :hd] = dk_scr[:, half:].T * scale
        keep_ref[:, hd:] = dv_scr[:, half:].T


def attention(queries, kv_prev, kv_own, grad_ctx, rel_start):
    rows, hd = queries.shape
    tq = 256
    window = rows + tq
    kernel = functools.partial(
        attention_kernel, tq=tq, window=window, shift=rows, scale=hd ** (-0.5)
    )
    q_spec = pl.BlockSpec((tq, hd), lambda i: (i, 0))
    k_spec = pl.BlockSpec((rows, hd), lambda i: (0, 0))
    v_spec = pl.BlockSpec((rows, hd), lambda i: (0, 1))
    kv_spec = pl.BlockSpec((rows, 2 * hd), lambda i: (0, 0))
    steps = rows // tq
    cost = pl.CostEstimate(
        flops=steps * 12 * tq * window * hd,
        transcendentals=steps * 2 * tq * window,
        bytes_accessed=rows * hd * 2 * 8 + rows * 2 * hd * 6,
    )
    return pl.pallas_call(
        kernel,
        grid=(steps,),
        in_specs=[q_spec, k_spec, v_spec, k_spec, v_spec, q_spec,
                  pl.BlockSpec((tq, 1), lambda i: (i, 0))],
        out_specs=[q_spec, q_spec, kv_spec, kv_spec],
        out_shape=[
            jax.ShapeDtypeStruct((rows, hd), jnp.bfloat16),
            jax.ShapeDtypeStruct((rows, hd), jnp.bfloat16),
            jax.ShapeDtypeStruct((rows, 2 * hd), jnp.bfloat16),
            jax.ShapeDtypeStruct((rows, 2 * hd), jnp.float32),
        ],
        scratch_shapes=[pltpu.VMEM((2 * rows, hd), jnp.bfloat16)]
        + [pltpu.VMEM((hd, 2 * rows), jnp.bfloat16)] * 2
        + [pltpu.VMEM((hd, 2 * rows), jnp.float32)] * 2,
        compiler_params=pltpu.CompilerParams(dimension_semantics=("arbitrary",)),
        cost_estimate=cost,
    )(queries, kv_prev, kv_prev, kv_own, kv_own, grad_ctx, rel_start)


def body(
    own_rows, gain, w_query, w_key, w_value, grad_context, send_slot, recv_slot, episode_start
):
    seq_count = lax.axis_size("seq")
    head_count = lax.axis_size("head")
    shard = lax.axis_index("seq")
    head_pos = lax.axis_index("head")
    row_count = own_rows.shape[0]
    capacity = 2 * row_count // seq_count
    width = own_rows.shape[1] // head_count
    own_part = lax.dynamic_slice_in_dim(own_rows, head_pos * width, width, 1)
    slots = seq_count * capacity
    send_pick = (
        lax.broadcasted_iota(jnp.int32, (slots, row_count), 0) == send_slot[None, :]
    ).astype(own_rows.dtype)
    outgoing = jnp.dot(send_pick, own_part, preferred_element_type=jnp.float32).astype(
        own_rows.dtype
    )
    arrived = lax.all_to_all(outgoing, "seq", split_axis=0, concat_axis=0, tiled=True)
    recv_pick = (
        lax.broadcasted_iota(jnp.int32, (row_count, slots), 1) == recv_slot[:, None]
    ).astype(own_rows.dtype)
    packed_part = jnp.dot(recv_pick, arrived, preferred_element_type=jnp.float32).astype(
        own_rows.dtype
    )
    packed = lax.all_gather(packed_part, "head", axis=1, tiled=True)
    rows_float = packed.astype(jnp.float32)
    inv_rms = lax.rsqrt(jnp.mean(rows_float * rows_float, axis=-1, keepdims=True) + epsilon)
    normed = (rows_float * inv_rms * gain).astype(jnp.bfloat16)
    queries = jnp.dot(normed, w_query, preferred_element_type=jnp.float32).astype(jnp.bfloat16)
    rel_start = (episode_start - (shard - 1) * row_count).reshape(row_count, 1)
    local_heads = queries.shape[1] // HD
    contexts, grad_queries, kv_parts = [], [], []
    for h in range(local_heads):
        cols = slice(h * HD, (h + 1) * HD)
        kv_weight = jnp.concatenate([w_key[:, cols], w_value[:, cols]], axis=1)
        kv_own = jnp.dot(normed, kv_weight, preferred_element_type=jnp.float32).astype(jnp.bfloat16)
        kv_sent = kv_own
        if h > 0:
            kv_sent, _ = lax.optimization_barrier((kv_own, kv_prev))
        kv_prev = passed_along(kv_sent, "seq", 1)
        context_h, grad_q_h, kv_send, kv_keep = attention(
            queries[:, cols], kv_prev, kv_own, grad_context[:, cols], rel_start
        )
        kv_next = passed_along(kv_send, "seq", -1)
        grad_kv = (kv_keep + kv_next.astype(jnp.float32)).astype(jnp.bfloat16)
        contexts.append(context_h)
        grad_queries.append(grad_q_h)
        kv_parts.append((grad_kv, kv_weight))
    context_out = jnp.concatenate(contexts, axis=1)
    grad_q_all = jnp.concatenate(grad_queries, axis=1)
    share = row_count // head_count

    def project(grads, weight):
        return jnp.einsum("rc,dc->rd", grads, weight, preferred_element_type=jnp.float32)

    term = project(grad_q_all, w_query)
    for grad_kv, kv_weight in kv_parts:
        term = term + project(grad_kv, kv_weight)
    grad_normed = lax.psum_scatter(
        term.astype(jnp.bfloat16),
        "head",
        scatter_dimension=0,
        tiled=True,
    ).astype(jnp.float32)
    own_start = head_pos * share
    mine = lax.dynamic_slice_in_dim(packed, own_start, share, 0).astype(jnp.float32)
    mine_inv = lax.dynamic_slice_in_dim(inv_rms, own_start, share, 0)
    mine, mine_inv, mine_cubed = lax.optimization_barrier((mine, mine_inv, mine * mine_inv**3))
    gain_grad = gain * grad_normed
    mixed = jnp.mean(gain_grad * mine, axis=-1, keepdims=True)
    d_rows = (mine_inv * gain_grad - mine_cubed * mixed).astype(jnp.bfloat16)
    return (context_out, d_rows)


def solution(mesh):
    in_specs = (
        P("seq", None),
        P(),
        P(None, "head"),
        P(None, "head"),
        P(None, "head"),
        P("seq", "head"),
        P("seq"),
        P("seq"),
        P("seq"),
    )
    out_specs = (P("seq", "head"), P(("seq", "head"), None))
    return jax.shard_map(body, mesh=mesh, in_specs=in_specs, out_specs=out_specs, check_vma=False)
```

```python
import functools

import jax
import jax.numpy as jnp
from jax import lax
from jax.experimental import pallas as pl
from jax.experimental.pallas import tpu as pltpu
from jax.sharding import PartitionSpec as P

HD = 128


neg_large = -1e30
epsilon = 1e-05


def passed_along(array, axis, by):
    count = lax.axis_size(axis)
    pairs = [(i, i + by) for i in range(count) if 0 <= i + by < count]
    return lax.ppermute(array, axis, pairs)


def block_terms(queries, keys_all, values_all, grad_ctx, starts, first_query, first_key):
    score_scale = queries.shape[-1] ** (-0.5)
    query_pos = first_query + jnp.arange(queries.shape[0], dtype=jnp.int32)
    key_pos = first_key + jnp.arange(keys_all.shape[0], dtype=jnp.int32)
    allowed = (key_pos[None, :] >= starts[:, None]) & (key_pos[None, :] <= query_pos[:, None])
    scores = (
        jnp.einsum("bhe,khe->bhk", queries, keys_all, preferred_element_type=jnp.float32)
        * score_scale
    )
    scores = jnp.where(allowed[:, None, :], scores, neg_large)
    row_top = jnp.max(scores, axis=-1, keepdims=True)
    log_total = row_top + jnp.log(jnp.sum(jnp.exp(scores - row_top), axis=-1, keepdims=True))
    probs = jnp.exp(scores - log_total)
    probs_low = probs.astype(jnp.bfloat16)
    context = jnp.einsum("bhk,khe->bhe", probs_low, values_all, preferred_element_type=jnp.float32)
    grad_probs = jnp.einsum(
        "bhe,khe->bhk", grad_ctx, values_all, preferred_element_type=jnp.float32
    )
    weighted = jnp.sum(probs * grad_probs, axis=-1, keepdims=True)
    grad_scores = (probs * (grad_probs - weighted)).astype(jnp.bfloat16)
    grad_q = (
        jnp.einsum("bhk,khe->bhe", grad_scores, keys_all, preferred_element_type=jnp.float32)
        * score_scale
    )
    grad_k = (
        jnp.einsum("bhk,bhe->khe", grad_scores, queries, preferred_element_type=jnp.float32)
        * score_scale
    )
    grad_v = jnp.einsum("bhk,bhe->khe", probs_low, grad_ctx, preferred_element_type=jnp.float32)
    return (context, grad_q, grad_k, grad_v)


def attention_kernel(
    q_ref, kp_ref, vp_ref, ko_ref, vo_ref, do_ref, st_ref,
    ctx_ref, dq_ref, send_ref, keep_ref,
    k_scr, kt_scr, vt_scr, dk_scr, dv_scr, *, tq, window, shift, scale
):
    qi = pl.program_id(0)
    a = pl.multiple_of(qi * tq, tq)
    half = kp_ref.shape[0]

    @pl.when(qi == 0)
    def _():
        k_scr[:half, :] = kp_ref[...]
        k_scr[half:, :] = ko_ref[...]
        kt_scr[:, :half] = kp_ref[...].T
        kt_scr[:, half:] = ko_ref[...].T
        vt_scr[:, :half] = vp_ref[...].T
        vt_scr[:, half:] = vo_ref[...].T
        dk_scr[...] = jnp.zeros_like(dk_scr)
        dv_scr[...] = jnp.zeros_like(dv_scr)

    q = q_ref[...]
    k = k_scr[pl.ds(a, window), :]
    kt = kt_scr[:, pl.ds(a, window)]
    vt = vt_scr[:, pl.ds(a, window)]
    do = do_ref[...]
    s = jnp.dot(q, kt, preferred_element_type=jnp.float32) * scale
    key_off = lax.broadcasted_iota(jnp.int32, (tq, window), 1)
    row_off = lax.broadcasted_iota(jnp.int32, (tq, window), 0)
    allowed = (key_off >= st_ref[...] - a) & (key_off - row_off <= shift)
    s = jnp.where(allowed, s, neg_large)
    row_top = jnp.max(s, axis=1, keepdims=True)
    log_total = row_top + jnp.log(jnp.sum(jnp.exp(s - row_top), axis=1, keepdims=True))
    p = jnp.exp(s - log_total)
    p_low = p.astype(jnp.bfloat16)
    ctx_ref[...] = lax.dot_general(
        p_low, vt, (((1,), (1,)), ((), ())), preferred_element_type=jnp.float32
    ).astype(ctx_ref.dtype)
    dp = jnp.dot(do, vt, preferred_element_type=jnp.float32)
    weighted = jnp.sum(p * dp, axis=1, keepdims=True)
    ds = (p * (dp - weighted)).astype(jnp.bfloat16)
    dq_ref[...] = (jnp.dot(ds, k, preferred_element_type=jnp.float32) * scale).astype(dq_ref.dtype)
    dk_scr[:, pl.ds(a, window)] += jnp.dot(q.T, ds, preferred_element_type=jnp.float32)
    dv_scr[:, pl.ds(a, window)] += jnp.dot(do.T, p_low, preferred_element_type=jnp.float32)

    @pl.when(qi == pl.num_programs(0) - 1)
    def _():
        hd = q_ref.shape[1]
        send_ref[:, :hd] = (dk_scr[:, :half].T * scale).astype(send_ref.dtype)
        send_ref[:, hd:] = dv_scr[:, :half].T.astype(send_ref.dtype)
        keep_ref[:, :hd] = dk_scr[:, half:].T * scale
        keep_ref[:, hd:] = dv_scr[:, half:].T


def attention(queries, kv_prev, kv_own, grad_ctx, rel_start):
    rows, hd = queries.shape
    tq = 512
    window = rows + tq
    kernel = functools.partial(
        attention_kernel, tq=tq, window=window, shift=rows, scale=hd ** (-0.5)
    )
    q_spec = pl.BlockSpec((tq, hd), lambda i: (i, 0))
    k_spec = pl.BlockSpec((rows, hd), lambda i: (0, 0))
    v_spec = pl.BlockSpec((rows, hd), lambda i: (0, 1))
    kv_spec = pl.BlockSpec((rows, 2 * hd), lambda i: (0, 0))
    steps = rows // tq
    cost = pl.CostEstimate(
        flops=steps * 12 * tq * window * hd,
        transcendentals=steps * 2 * tq * window,
        bytes_accessed=rows * hd * 2 * 8 + rows * 2 * hd * 6,
    )
    return pl.pallas_call(
        kernel,
        grid=(steps,),
        in_specs=[q_spec, k_spec, v_spec, k_spec, v_spec, q_spec,
                  pl.BlockSpec((tq, 1), lambda i: (i, 0))],
        out_specs=[q_spec, q_spec, kv_spec, kv_spec],
        out_shape=[
            jax.ShapeDtypeStruct((rows, hd), jnp.bfloat16),
            jax.ShapeDtypeStruct((rows, hd), jnp.bfloat16),
            jax.ShapeDtypeStruct((rows, 2 * hd), jnp.bfloat16),
            jax.ShapeDtypeStruct((rows, 2 * hd), jnp.float32),
        ],
        scratch_shapes=[pltpu.VMEM((2 * rows, hd), jnp.bfloat16)]
        + [pltpu.VMEM((hd, 2 * rows), jnp.bfloat16)] * 2
        + [pltpu.VMEM((hd, 2 * rows), jnp.float32)] * 2,
        compiler_params=pltpu.CompilerParams(dimension_semantics=("arbitrary",)),
        cost_estimate=cost,
    )(queries, kv_prev, kv_prev, kv_own, kv_own, grad_ctx, rel_start)


def body(
    own_rows, gain, w_query, w_key, w_value, grad_context, send_slot, recv_slot, episode_start
):
    seq_count = lax.axis_size("seq")
    head_count = lax.axis_size("head")
    shard = lax.axis_index("seq")
    head_pos = lax.axis_index("head")
    row_count = own_rows.shape[0]
    capacity = 2 * row_count // seq_count
    width = own_rows.shape[1] // head_count
    own_part = lax.dynamic_slice_in_dim(own_rows, head_pos * width, width, 1)
    slots = seq_count * capacity
    send_pick = (
        lax.broadcasted_iota(jnp.int32, (slots, row_count), 0) == send_slot[None, :]
    ).astype(own_rows.dtype)
    outgoing = jnp.dot(send_pick, own_part, preferred_element_type=jnp.float32).astype(
        own_rows.dtype
    )
    arrived = lax.all_to_all(outgoing, "seq", split_axis=0, concat_axis=0, tiled=True)
    recv_pick = (
        lax.broadcasted_iota(jnp.int32, (row_count, slots), 1) == recv_slot[:, None]
    ).astype(own_rows.dtype)
    packed_part = jnp.dot(recv_pick, arrived, preferred_element_type=jnp.float32).astype(
        own_rows.dtype
    )
    packed = lax.all_gather(packed_part, "head", axis=1, tiled=True)
    rows_float = packed.astype(jnp.float32)
    inv_rms = lax.rsqrt(jnp.mean(rows_float * rows_float, axis=-1, keepdims=True) + epsilon)
    normed = (rows_float * inv_rms * gain).astype(jnp.bfloat16)
    queries = jnp.dot(normed, w_query, preferred_element_type=jnp.float32).astype(jnp.bfloat16)
    rel_start = (episode_start - (shard - 1) * row_count).reshape(row_count, 1)
    local_heads = queries.shape[1] // HD
    contexts, grad_queries, kv_parts = [], [], []
    for h in range(local_heads):
        cols = slice(h * HD, (h + 1) * HD)
        kv_weight = jnp.concatenate([w_key[:, cols], w_value[:, cols]], axis=1)
        kv_own = jnp.dot(normed, kv_weight, preferred_element_type=jnp.float32).astype(jnp.bfloat16)
        kv_sent = kv_own
        if h > 0:
            kv_sent, _ = lax.optimization_barrier((kv_own, kv_prev))
        kv_prev = passed_along(kv_sent, "seq", 1)
        context_h, grad_q_h, kv_send, kv_keep = attention(
            queries[:, cols], kv_prev, kv_own, grad_context[:, cols], rel_start
        )
        kv_next = passed_along(kv_send, "seq", -1)
        grad_kv = (kv_keep + kv_next.astype(jnp.float32)).astype(jnp.bfloat16)
        contexts.append(context_h)
        grad_queries.append(grad_q_h)
        kv_parts.append((grad_kv, kv_weight))
    context_out = jnp.concatenate(contexts, axis=1)
    grad_q_all = jnp.concatenate(grad_queries, axis=1)
    share = row_count // head_count

    def project(grads, weight):
        return jnp.einsum("rc,dc->rd", grads, weight, preferred_element_type=jnp.float32)

    term = project(grad_q_all, w_query)
    for grad_kv, kv_weight in kv_parts:
        term = term + project(grad_kv, kv_weight)
    grad_normed = lax.psum_scatter(
        term.astype(jnp.bfloat16),
        "head",
        scatter_dimension=0,
        tiled=True,
    ).astype(jnp.float32)
    own_start = head_pos * share
    mine = lax.dynamic_slice_in_dim(packed, own_start, share, 0).astype(jnp.float32)
    mine_inv = lax.dynamic_slice_in_dim(inv_rms, own_start, share, 0)
    gain_grad = gain * grad_normed
    mixed = jnp.mean(gain_grad * mine, axis=-1, keepdims=True)
    d_rows = (mine_inv * gain_grad - mine * mine_inv**3 * mixed).astype(jnp.bfloat16)
    return (context_out, d_rows)


def solution(mesh):
    in_specs = (
        P("seq", None),
        P(),
        P(None, "head"),
        P(None, "head"),
        P(None, "head"),
        P("seq", "head"),
        P("seq"),
        P("seq"),
        P("seq"),
    )
    out_specs = (P("seq", "head"), P(("seq", "head"), None))
    return jax.shard_map(body, mesh=mesh, in_specs=in_specs, out_specs=out_specs, check_vma=False)
```

```python
import functools

import jax
import jax.numpy as jnp
from jax import lax
from jax.experimental import pallas as pl
from jax.experimental.pallas import tpu as pltpu
from jax.sharding import PartitionSpec as P

HD = 128


neg_large = -1e30
epsilon = 1e-05


def passed_along(array, axis, by):
    count = lax.axis_size(axis)
    pairs = [(i, i + by) for i in range(count) if 0 <= i + by < count]
    return lax.ppermute(array, axis, pairs)


def block_terms(queries, keys_all, values_all, grad_ctx, starts, first_query, first_key):
    score_scale = queries.shape[-1] ** (-0.5)
    query_pos = first_query + jnp.arange(queries.shape[0], dtype=jnp.int32)
    key_pos = first_key + jnp.arange(keys_all.shape[0], dtype=jnp.int32)
    allowed = (key_pos[None, :] >= starts[:, None]) & (key_pos[None, :] <= query_pos[:, None])
    scores = (
        jnp.einsum("bhe,khe->bhk", queries, keys_all, preferred_element_type=jnp.float32)
        * score_scale
    )
    scores = jnp.where(allowed[:, None, :], scores, neg_large)
    row_top = jnp.max(scores, axis=-1, keepdims=True)
    log_total = row_top + jnp.log(jnp.sum(jnp.exp(scores - row_top), axis=-1, keepdims=True))
    probs = jnp.exp(scores - log_total)
    probs_low = probs.astype(jnp.bfloat16)
    context = jnp.einsum("bhk,khe->bhe", probs_low, values_all, preferred_element_type=jnp.float32)
    grad_probs = jnp.einsum(
        "bhe,khe->bhk", grad_ctx, values_all, preferred_element_type=jnp.float32
    )
    weighted = jnp.sum(probs * grad_probs, axis=-1, keepdims=True)
    grad_scores = (probs * (grad_probs - weighted)).astype(jnp.bfloat16)
    grad_q = (
        jnp.einsum("bhk,khe->bhe", grad_scores, keys_all, preferred_element_type=jnp.float32)
        * score_scale
    )
    grad_k = (
        jnp.einsum("bhk,bhe->khe", grad_scores, queries, preferred_element_type=jnp.float32)
        * score_scale
    )
    grad_v = jnp.einsum("bhk,bhe->khe", probs_low, grad_ctx, preferred_element_type=jnp.float32)
    return (context, grad_q, grad_k, grad_v)


def attention_kernel(
    q_ref, kp_ref, vp_ref, ko_ref, vo_ref, do_ref, st_ref,
    ctx_ref, dq_ref, send_ref, keep_ref,
    k_scr, kt_scr, vt_scr, dk_scr, dv_scr, *, tq, window, shift, scale
):
    qi = pl.program_id(0)
    a = pl.multiple_of(qi * tq, tq)
    half = kp_ref.shape[0]

    @pl.when(qi == 0)
    def _():
        k_scr[:half, :] = kp_ref[...]
        k_scr[half:, :] = ko_ref[...]
        kt_scr[:, :half] = kp_ref[...].T
        kt_scr[:, half:] = ko_ref[...].T
        vt_scr[:, :half] = vp_ref[...].T
        vt_scr[:, half:] = vo_ref[...].T
        dk_scr[...] = jnp.zeros_like(dk_scr)
        dv_scr[...] = jnp.zeros_like(dv_scr)

    q = q_ref[...]
    k = k_scr[pl.ds(a, window), :]
    kt = kt_scr[:, pl.ds(a, window)]
    vt = vt_scr[:, pl.ds(a, window)]
    do = do_ref[...]
    s = jnp.dot(q, kt, preferred_element_type=jnp.float32) * scale
    key_off = lax.broadcasted_iota(jnp.int32, (tq, window), 1)
    row_off = lax.broadcasted_iota(jnp.int32, (tq, window), 0)
    allowed = (key_off >= st_ref[...] - a) & (key_off - row_off <= shift)
    s = jnp.where(allowed, s, neg_large)
    row_top = jnp.max(s, axis=1, keepdims=True)
    log_total = row_top + jnp.log(jnp.sum(jnp.exp(s - row_top), axis=1, keepdims=True))
    p = jnp.exp(s - log_total)
    p_low = p.astype(jnp.bfloat16)
    ctx_ref[...] = lax.dot_general(
        p_low, vt, (((1,), (1,)), ((), ())), preferred_element_type=jnp.float32
    ).astype(ctx_ref.dtype)
    dp = jnp.dot(do, vt, preferred_element_type=jnp.float32)
    weighted = jnp.sum(p * dp, axis=1, keepdims=True)
    ds = (p * (dp - weighted)).astype(jnp.bfloat16)
    dq_ref[...] = (jnp.dot(ds, k, preferred_element_type=jnp.float32) * scale).astype(dq_ref.dtype)
    dk_scr[:, pl.ds(a, window)] += jnp.dot(q.T, ds, preferred_element_type=jnp.float32)
    dv_scr[:, pl.ds(a, window)] += jnp.dot(do.T, p_low, preferred_element_type=jnp.float32)

    @pl.when(qi == pl.num_programs(0) - 1)
    def _():
        hd = q_ref.shape[1]
        send_ref[:, :hd] = (dk_scr[:, :half].T * scale).astype(send_ref.dtype)
        send_ref[:, hd:] = dv_scr[:, :half].T.astype(send_ref.dtype)
        keep_ref[:, :hd] = dk_scr[:, half:].T * scale
        keep_ref[:, hd:] = dv_scr[:, half:].T


def attention(queries, kv_prev, kv_own, grad_ctx, rel_start):
    rows, hd = queries.shape
    tq = 512
    window = rows + tq
    kernel = functools.partial(
        attention_kernel, tq=tq, window=window, shift=rows, scale=hd ** (-0.5)
    )
    q_spec = pl.BlockSpec((tq, hd), lambda i: (i, 0))
    k_spec = pl.BlockSpec((rows, hd), lambda i: (0, 0))
    v_spec = pl.BlockSpec((rows, hd), lambda i: (0, 1))
    kv_spec = pl.BlockSpec((rows, 2 * hd), lambda i: (0, 0))
    steps = rows // tq
    cost = pl.CostEstimate(
        flops=steps * 12 * tq * window * hd,
        transcendentals=steps * 2 * tq * window,
        bytes_accessed=rows * hd * 2 * 8 + rows * 2 * hd * 6,
    )
    return pl.pallas_call(
        kernel,
        grid=(steps,),
        in_specs=[q_spec, k_spec, v_spec, k_spec, v_spec, q_spec,
                  pl.BlockSpec((tq, 1), lambda i: (i, 0))],
        out_specs=[q_spec, q_spec, kv_spec, kv_spec],
        out_shape=[
            jax.ShapeDtypeStruct((rows, hd), jnp.bfloat16),
            jax.ShapeDtypeStruct((rows, hd), jnp.bfloat16),
            jax.ShapeDtypeStruct((rows, 2 * hd), jnp.bfloat16),
            jax.ShapeDtypeStruct((rows, 2 * hd), jnp.float32),
        ],
        scratch_shapes=[pltpu.VMEM((2 * rows, hd), jnp.bfloat16)]
        + [pltpu.VMEM((hd, 2 * rows), jnp.bfloat16)] * 2
        + [pltpu.VMEM((hd, 2 * rows), jnp.float32)] * 2,
        compiler_params=pltpu.CompilerParams(dimension_semantics=("arbitrary",)),
        cost_estimate=cost,
    )(queries, kv_prev, kv_prev, kv_own, kv_own, grad_ctx, rel_start)


def body(
    own_rows, gain, w_query, w_key, w_value, grad_context, send_slot, recv_slot, episode_start
):
    seq_count = lax.axis_size("seq")
    head_count = lax.axis_size("head")
    shard = lax.axis_index("seq")
    head_pos = lax.axis_index("head")
    row_count = own_rows.shape[0]
    capacity = 2 * row_count // seq_count
    width = own_rows.shape[1] // head_count
    own_part = lax.dynamic_slice_in_dim(own_rows, head_pos * width, width, 1)
    slots = seq_count * capacity
    send_pick = (
        lax.broadcasted_iota(jnp.int32, (slots, row_count), 0) == send_slot[None, :]
    ).astype(own_rows.dtype)
    outgoing = jnp.dot(send_pick, own_part, preferred_element_type=jnp.float32).astype(
        own_rows.dtype
    )
    arrived = lax.all_to_all(outgoing, "seq", split_axis=0, concat_axis=0, tiled=True)
    recv_pick = (
        lax.broadcasted_iota(jnp.int32, (row_count, slots), 1) == recv_slot[:, None]
    ).astype(own_rows.dtype)
    packed_part = jnp.dot(recv_pick, arrived, preferred_element_type=jnp.float32).astype(
        own_rows.dtype
    )
    packed = lax.all_gather(packed_part, "head", axis=1, tiled=True)
    rows_float = packed.astype(jnp.float32)
    inv_rms = lax.rsqrt(jnp.mean(rows_float * rows_float, axis=-1, keepdims=True) + epsilon)
    normed = (rows_float * inv_rms * gain).astype(jnp.bfloat16)
    queries = jnp.dot(normed, w_query, preferred_element_type=jnp.float32).astype(jnp.bfloat16)
    rel_start = (episode_start - (shard - 1) * row_count).reshape(row_count, 1)
    local_heads = queries.shape[1] // HD
    contexts, grad_queries, kv_parts = [], [], []
    for h in range(local_heads):
        cols = slice(h * HD, (h + 1) * HD)
        kv_weight = jnp.concatenate([w_key[:, cols], w_value[:, cols]], axis=1)
        kv_own = jnp.dot(normed, kv_weight, preferred_element_type=jnp.float32).astype(jnp.bfloat16)
        kv_sent = kv_own
        if h > 0:
            kv_sent, _ = lax.optimization_barrier((kv_own, kv_prev))
        kv_prev = passed_along(kv_sent, "seq", 1)
        context_h, grad_q_h, kv_send, kv_keep = attention(
            queries[:, cols], kv_prev, kv_own, grad_context[:, cols], rel_start
        )
        kv_next = passed_along(kv_send, "seq", -1)
        grad_kv = (kv_keep + kv_next.astype(jnp.float32)).astype(jnp.bfloat16)
        contexts.append(context_h)
        grad_queries.append(grad_q_h)
        kv_parts.append((grad_kv, kv_weight))
    context_out = jnp.concatenate(contexts, axis=1)
    grad_q_all = jnp.concatenate(grad_queries, axis=1)
    share = row_count // head_count

    def project(grads, weight):
        return jnp.einsum("rc,dc->rd", grads, weight, preferred_element_type=jnp.float32)

    term = project(grad_q_all, w_query)
    for grad_kv, kv_weight in kv_parts[:-1]:
        term = term + project(grad_kv, kv_weight)
    term = lax.optimization_barrier(term)
    term = term + project(kv_parts[-1][0], kv_parts[-1][1])
    grad_normed = lax.psum_scatter(
        term.astype(jnp.bfloat16),
        "head",
        scatter_dimension=0,
        tiled=True,
    ).astype(jnp.float32)
    own_start = head_pos * share
    mine = lax.dynamic_slice_in_dim(packed, own_start, share, 0).astype(jnp.float32)
    mine_inv = lax.dynamic_slice_in_dim(inv_rms, own_start, share, 0)
    gain_grad = gain * grad_normed
    mixed = jnp.mean(gain_grad * mine, axis=-1, keepdims=True)
    d_rows = (mine_inv * gain_grad - mine * mine_inv**3 * mixed).astype(jnp.bfloat16)
    return (context_out, d_rows)


def solution(mesh):
    in_specs = (
        P("seq", None),
        P(),
        P(None, "head"),
        P(None, "head"),
        P(None, "head"),
        P("seq", "head"),
        P("seq"),
        P("seq"),
        P("seq"),
    )
    out_specs = (P("seq", "head"), P(("seq", "head"), None))
    return jax.shard_map(body, mesh=mesh, in_specs=in_specs, out_specs=out_specs, check_vma=False)
```

```python
import functools

import jax
import jax.numpy as jnp
from jax import lax
from jax.experimental import pallas as pl
from jax.experimental.pallas import tpu as pltpu
from jax.sharding import PartitionSpec as P

HD = 128


neg_large = -1e30
epsilon = 1e-05


def passed_along(array, axis, by):
    count = lax.axis_size(axis)
    pairs = [(i, i + by) for i in range(count) if 0 <= i + by < count]
    return lax.ppermute(array, axis, pairs)


def block_terms(queries, keys_all, values_all, grad_ctx, starts, first_query, first_key):
    score_scale = queries.shape[-1] ** (-0.5)
    query_pos = first_query + jnp.arange(queries.shape[0], dtype=jnp.int32)
    key_pos = first_key + jnp.arange(keys_all.shape[0], dtype=jnp.int32)
    allowed = (key_pos[None, :] >= starts[:, None]) & (key_pos[None, :] <= query_pos[:, None])
    scores = (
        jnp.einsum("bhe,khe->bhk", queries, keys_all, preferred_element_type=jnp.float32)
        * score_scale
    )
    scores = jnp.where(allowed[:, None, :], scores, neg_large)
    row_top = jnp.max(scores, axis=-1, keepdims=True)
    log_total = row_top + jnp.log(jnp.sum(jnp.exp(scores - row_top), axis=-1, keepdims=True))
    probs = jnp.exp(scores - log_total)
    probs_low = probs.astype(jnp.bfloat16)
    context = jnp.einsum("bhk,khe->bhe", probs_low, values_all, preferred_element_type=jnp.float32)
    grad_probs = jnp.einsum(
        "bhe,khe->bhk", grad_ctx, values_all, preferred_element_type=jnp.float32
    )
    weighted = jnp.sum(probs * grad_probs, axis=-1, keepdims=True)
    grad_scores = (probs * (grad_probs - weighted)).astype(jnp.bfloat16)
    grad_q = (
        jnp.einsum("bhk,khe->bhe", grad_scores, keys_all, preferred_element_type=jnp.float32)
        * score_scale
    )
    grad_k = (
        jnp.einsum("bhk,bhe->khe", grad_scores, queries, preferred_element_type=jnp.float32)
        * score_scale
    )
    grad_v = jnp.einsum("bhk,bhe->khe", probs_low, grad_ctx, preferred_element_type=jnp.float32)
    return (context, grad_q, grad_k, grad_v)


def attention_kernel(
    q_ref, kp_ref, vp_ref, ko_ref, vo_ref, do_ref, st_ref,
    ctx_ref, dq_ref, send_ref, keep_ref,
    k_scr, kt_scr, vt_scr, dk_scr, dv_scr, *, tq, window, shift, scale
):
    qi = pl.program_id(0)
    a = pl.multiple_of(qi * tq, tq)
    half = kp_ref.shape[0]

    @pl.when(qi == 0)
    def _():
        k_scr[:half, :] = kp_ref[...]
        k_scr[half:, :] = ko_ref[...]
        kt_scr[:, :half] = kp_ref[...].T
        kt_scr[:, half:] = ko_ref[...].T
        vt_scr[:, :half] = vp_ref[...].T
        vt_scr[:, half:] = vo_ref[...].T
        dk_scr[...] = jnp.zeros_like(dk_scr)
        dv_scr[...] = jnp.zeros_like(dv_scr)

    q = q_ref[...]
    k = k_scr[pl.ds(a, window), :]
    kt = kt_scr[:, pl.ds(a, window)]
    vt = vt_scr[:, pl.ds(a, window)]
    do = do_ref[...]
    s = jnp.dot(q, kt, preferred_element_type=jnp.float32) * scale
    key_off = lax.broadcasted_iota(jnp.int32, (tq, window), 1)
    row_off = lax.broadcasted_iota(jnp.int32, (tq, window), 0)
    allowed = (key_off >= st_ref[...] - a) & (key_off - row_off <= shift)
    s = jnp.where(allowed, s, neg_large)
    row_top = jnp.max(s, axis=1, keepdims=True)
    e = jnp.exp(s - row_top)
    p = e * (1.0 / jnp.sum(e, axis=1, keepdims=True))
    p_low = p.astype(jnp.bfloat16)
    ctx_ref[...] = lax.dot_general(
        p_low, vt, (((1,), (1,)), ((), ())), preferred_element_type=jnp.float32
    ).astype(ctx_ref.dtype)
    dp = jnp.dot(do, vt, preferred_element_type=jnp.float32)
    weighted = jnp.sum(p * dp, axis=1, keepdims=True)
    ds = (p * (dp - weighted)).astype(jnp.bfloat16)
    dq_ref[...] = (jnp.dot(ds, k, preferred_element_type=jnp.float32) * scale).astype(dq_ref.dtype)
    dk_scr[:, pl.ds(a, window)] += jnp.dot(q.T, ds, preferred_element_type=jnp.float32)
    dv_scr[:, pl.ds(a, window)] += jnp.dot(do.T, p_low, preferred_element_type=jnp.float32)

    @pl.when(qi == pl.num_programs(0) - 1)
    def _():
        hd = q_ref.shape[1]
        send_ref[:, :hd] = (dk_scr[:, :half].T * scale).astype(send_ref.dtype)
        send_ref[:, hd:] = dv_scr[:, :half].T.astype(send_ref.dtype)
        keep_ref[:, :hd] = dk_scr[:, half:].T * scale
        keep_ref[:, hd:] = dv_scr[:, half:].T


def attention(queries, kv_prev, kv_own, grad_ctx, rel_start):
    rows, hd = queries.shape
    tq = 512
    window = rows + tq
    kernel = functools.partial(
        attention_kernel, tq=tq, window=window, shift=rows, scale=hd ** (-0.5)
    )
    q_spec = pl.BlockSpec((tq, hd), lambda i: (i, 0))
    k_spec = pl.BlockSpec((rows, hd), lambda i: (0, 0))
    v_spec = pl.BlockSpec((rows, hd), lambda i: (0, 1))
    kv_spec = pl.BlockSpec((rows, 2 * hd), lambda i: (0, 0))
    steps = rows // tq
    cost = pl.CostEstimate(
        flops=steps * 12 * tq * window * hd,
        transcendentals=steps * 2 * tq * window,
        bytes_accessed=rows * hd * 2 * 8 + rows * 2 * hd * 6,
    )
    return pl.pallas_call(
        kernel,
        grid=(steps,),
        in_specs=[q_spec, k_spec, v_spec, k_spec, v_spec, q_spec,
                  pl.BlockSpec((tq, 1), lambda i: (i, 0))],
        out_specs=[q_spec, q_spec, kv_spec, kv_spec],
        out_shape=[
            jax.ShapeDtypeStruct((rows, hd), jnp.bfloat16),
            jax.ShapeDtypeStruct((rows, hd), jnp.bfloat16),
            jax.ShapeDtypeStruct((rows, 2 * hd), jnp.bfloat16),
            jax.ShapeDtypeStruct((rows, 2 * hd), jnp.float32),
        ],
        scratch_shapes=[pltpu.VMEM((2 * rows, hd), jnp.bfloat16)]
        + [pltpu.VMEM((hd, 2 * rows), jnp.bfloat16)] * 2
        + [pltpu.VMEM((hd, 2 * rows), jnp.float32)] * 2,
        compiler_params=pltpu.CompilerParams(dimension_semantics=("arbitrary",)),
        cost_estimate=cost,
    )(queries, kv_prev, kv_prev, kv_own, kv_own, grad_ctx, rel_start)


def body(
    own_rows, gain, w_query, w_key, w_value, grad_context, send_slot, recv_slot, episode_start
):
    seq_count = lax.axis_size("seq")
    head_count = lax.axis_size("head")
    shard = lax.axis_index("seq")
    head_pos = lax.axis_index("head")
    row_count = own_rows.shape[0]
    capacity = 2 * row_count // seq_count
    width = own_rows.shape[1] // head_count
    own_part = lax.dynamic_slice_in_dim(own_rows, head_pos * width, width, 1)
    slots = seq_count * capacity
    send_pick = (
        lax.broadcasted_iota(jnp.int32, (slots, row_count), 0) == send_slot[None, :]
    ).astype(own_rows.dtype)
    outgoing = jnp.dot(send_pick, own_part, preferred_element_type=jnp.float32).astype(
        own_rows.dtype
    )
    arrived = lax.all_to_all(outgoing, "seq", split_axis=0, concat_axis=0, tiled=True)
    recv_pick = (
        lax.broadcasted_iota(jnp.int32, (row_count, slots), 1) == recv_slot[:, None]
    ).astype(own_rows.dtype)
    packed_part = jnp.dot(recv_pick, arrived, preferred_element_type=jnp.float32).astype(
        own_rows.dtype
    )
    packed = lax.all_gather(packed_part, "head", axis=1, tiled=True)
    rows_float = packed.astype(jnp.float32)
    inv_rms = lax.rsqrt(jnp.mean(rows_float * rows_float, axis=-1, keepdims=True) + epsilon)
    normed = (rows_float * inv_rms * gain).astype(jnp.bfloat16)
    queries = jnp.dot(normed, w_query, preferred_element_type=jnp.float32).astype(jnp.bfloat16)
    rel_start = (episode_start - (shard - 1) * row_count).reshape(row_count, 1)
    local_heads = queries.shape[1] // HD
    contexts, grad_queries, kv_parts = [], [], []
    for h in range(local_heads):
        cols = slice(h * HD, (h + 1) * HD)
        kv_weight = jnp.concatenate([w_key[:, cols], w_value[:, cols]], axis=1)
        kv_own = jnp.dot(normed, kv_weight, preferred_element_type=jnp.float32).astype(jnp.bfloat16)
        kv_sent = kv_own
        if h > 0:
            kv_sent, _ = lax.optimization_barrier((kv_own, kv_prev))
        kv_prev = passed_along(kv_sent, "seq", 1)
        context_h, grad_q_h, kv_send, kv_keep = attention(
            queries[:, cols], kv_prev, kv_own, grad_context[:, cols], rel_start
        )
        kv_next = passed_along(kv_send, "seq", -1)
        grad_kv = (kv_keep + kv_next.astype(jnp.float32)).astype(jnp.bfloat16)
        contexts.append(context_h)
        grad_queries.append(grad_q_h)
        kv_parts.append((grad_kv, kv_weight))
    context_out = jnp.concatenate(contexts, axis=1)
    grad_q_all = jnp.concatenate(grad_queries, axis=1)
    share = row_count // head_count

    def project(grads, weight):
        return jnp.einsum("rc,dc->rd", grads, weight, preferred_element_type=jnp.float32)

    term = project(grad_q_all, w_query)
    for grad_kv, kv_weight in kv_parts[:-1]:
        term = term + project(grad_kv, kv_weight)
    term = lax.optimization_barrier(term)
    term = term + project(kv_parts[-1][0], kv_parts[-1][1])
    grad_normed = lax.psum_scatter(
        term.astype(jnp.bfloat16),
        "head",
        scatter_dimension=0,
        tiled=True,
    ).astype(jnp.float32)
    own_start = head_pos * share
    mine = lax.dynamic_slice_in_dim(packed, own_start, share, 0).astype(jnp.float32)
    mine_inv = lax.dynamic_slice_in_dim(inv_rms, own_start, share, 0)
    gain_grad = gain * grad_normed
    mixed = jnp.mean(gain_grad * mine, axis=-1, keepdims=True)
    d_rows = (mine_inv * gain_grad - mine * mine_inv**3 * mixed).astype(jnp.bfloat16)
    return (context_out, d_rows)


def solution(mesh):
    in_specs = (
        P("seq", None),
        P(),
        P(None, "head"),
        P(None, "head"),
        P(None, "head"),
        P("seq", "head"),
        P("seq"),
        P("seq"),
        P("seq"),
    )
    out_specs = (P("seq", "head"), P(("seq", "head"), None))
    return jax.shard_map(body, mesh=mesh, in_specs=in_specs, out_specs=out_specs, check_vma=False)
```
